32 devices in a mesh: wave: 4 (over z), lev: 8 (over y, x, core).
Axes of the slice: x: 2, y: 2, z: 4, core: 2. Of those that a mesh axis runs over, the one named last changes fastest.
Arguments:
- spec: bfloat16 [1280, 2, 16, 1280], P('wave', None, 'lev'), may hold values from -0.119628906 to 0.119628906
- legendre: bfloat16 [1280, 16, 1280], P(('wave', 'lev')), may hold values from -0.15625 to 0.15625
- slot_wave: int32 [1280], replicated, may hold values from 0 to 1280, as said below
- row_lons: int32 [32], replicated, may hold values from 20 to 5136, as said below
- band_rows: int32 [32], replicated, may hold values from 0 to 31, as said below
Outputs:
- grid: float32 [32, 16, 5136], P('wave', 'lev')
The draws below stay inside these ranges and needn't reach their ends.
Inputs may be any that keep to these rules, and one draw needn't show every extreme that they name: `slot_wave`: every zonal wavenumber 0 to 1279 stands in exactly one slot; any other slot holds 1280. `row_lons`: row 16 + j has as many points as row j; each count is 20 plus a multiple of 4; some row has 5136. `band_rows`: a permutation of the latitude rows.
All inputs are finite; a program needn't handle non-finite values.
Results may differ from the reference program's by a relative error of at most 0.0037.
Values may be sent and summed in bfloat16 or wider, within the bound.
No kernel may reach another device: no remote copies, remote signals or barrier semaphores. Data moves between devices by JAX's collectives and lax.ppermute only.
A program may use at most 64 MiB of HBM per device.

```python
import math
import jax
import jax.numpy as jnp
from jax import lax

TRUNC = 1279
MW = 1280
FL = 16
NLATH = 16
ROWS = 32
SLOTS = 1280


def draw_slot_wave(key, part):
    perm = jax.random.permutation(key, SLOTS).astype(jnp.int32)
    return jnp.where(perm < MW, perm, MW).astype(jnp.int32)


def draw_row_lons(key, part):
    steps_north = jax.random.randint(key, (NLATH,), 0, MW).astype(jnp.int32)
    steps_north = steps_north.at[NLATH - 1].set(TRUNC)
    north = 20 + 4 * steps_north
    return jnp.concatenate([north, north]).astype(jnp.int32)


def draw_band_rows(key, part):
    return jax.random.permutation(key, ROWS).astype(jnp.int32)


def level_of(own_key, extent, shards, smallest, largest):
    loudness, own = 1.0, jax.random.fold_in(own_key, 6)
    for position, shards_of in shards:
        steps = jnp.exp(jax.random.uniform(jax.random.fold_in(own, position), (shards_of,), jnp.float32, smallest / len(shards), largest / len(shards)))
        loudness = loudness * jnp.repeat(steps, extent[position] // shards_of).reshape([-1 if axis == position else 1 for axis in range(len(extent))])
    return loudness


def scatter_about(key, extent, width, bound, shards=(), held_as=jnp.bfloat16):
    array = jax.random.normal(key, extent, jnp.float32) * width
    if len(shards) > 0:
        array = level_of(key, extent, shards, -0.22, 0.18) * array
    return jnp.clip(array, min=-bound, max=bound).astype(held_as)


def setup_inputs(seed: int = 0) -> dict:
    splits = jax.random.split(jax.random.key(seed), 6)
    spec = scatter_about(splits[0], (SLOTS, 2, FL, MW), 0.02, 0.119628906, ((0, 4), (2, 8)))
    legendre = scatter_about(splits[1], (SLOTS, NLATH, MW), MW ** -0.5, 0.15625, ((0, 32),))
    slot_wave = draw_slot_wave(jax.random.fold_in(splits[5], 71), 0)
    row_lons = draw_row_lons(jax.random.fold_in(splits[5], 71), 0)
    band_rows = draw_band_rows(jax.random.fold_in(splits[5], 71), 0)
    return {"spec": spec, "legendre": legendre, "slot_wave": slot_wave, "row_lons": row_lons, "band_rows": band_rows}


def angles(remainder, points):
    return (2.0 * math.pi) * remainder.astype(jnp.float32) / points.astype(jnp.float32)


def row_synthesis(coef_row, points):
    fields = coef_row.shape[1]
    waves = coef_row.shape[2]
    ablocks = waves // 64
    lon_len = 20 + 4 * (waves - 1)
    lon_idx = jnp.arange(lon_len, dtype=jnp.int32)
    inner = jnp.arange(64, dtype=jnp.int32)
    remainder = (inner[:, None] * lon_idx[None, :]) % points
    theta = angles(remainder, points)
    cosb = jnp.cos(theta).astype(jnp.bfloat16)
    sinb = jnp.sin(theta).astype(jnp.bfloat16)
    table = jnp.stack([jnp.stack([cosb, sinb], 1), jnp.stack([-sinb, cosb], 1)], 0)
    blocks = coef_row.reshape(2, fields, ablocks, 64)
    part = jnp.einsum("cfab,cbdi->dfai", blocks.astype(jnp.float32), table.astype(jnp.float32))
    outer = jnp.arange(ablocks, dtype=jnp.int32) * 64
    phase = angles((outer[:, None] * lon_idx[None, :]) % points, points)
    total = jnp.sum(part[0] * jnp.cos(phase)[None] - part[1] * jnp.sin(phase)[None], axis=1)
    return jnp.where(lon_idx[None, :] < points, total, jnp.zeros_like(total))


def slot_sums(item):
    coeffs, table, wave = item
    waves = coeffs.shape[-1]
    degree = jnp.arange(waves, dtype=jnp.int32)
    live_k = degree <= (waves - 1) - wave
    even_mask = live_k & (degree % 2 == 0)
    odd_mask = live_k & (degree % 2 == 1)
    zeros = jnp.zeros_like(coeffs)
    stacked = jnp.stack([jnp.where(even_mask, coeffs, zeros), jnp.where(odd_mask, coeffs, zeros)])
    return jnp.einsum("pcfk,jk->pcfj", stacked.astype(jnp.float32), table.astype(jnp.float32))


def reference(spec, legendre, slot_wave, row_lons, band_rows):
    waves = spec.shape[-1]
    nlath = legendre.shape[1]
    sums = lax.map(slot_sums, (spec, legendre, slot_wave))
    north = band_rows < nlath
    lat_idx = jnp.where(north, band_rows, band_rows - nlath).astype(jnp.int32)
    parity_sign = jnp.where(north, 1.0, -1.0).astype(jnp.float32)
    fourier = (sums[:, 0][..., lat_idx] + parity_sign * sums[:, 1][..., lat_idx]).astype(jnp.bfloat16)
    fourier_t = jnp.transpose(fourier, (1, 2, 3, 0))
    shape_full = fourier_t.shape[:3] + (waves + 1,)
    coef = jnp.zeros(shape_full, jnp.bfloat16).at[..., slot_wave].set(fourier_t)[..., :waves]
    wave_idx = jnp.arange(waves, dtype=jnp.int32)
    row_points = row_lons[band_rows]
    keep = 2 * wave_idx[None, :] < row_points[:, None]
    factor = jnp.where(keep, jnp.where(wave_idx[None, :] == 0, 1.0, 2.0), 0.0).astype(jnp.float32)
    coef = (coef.astype(jnp.float32) * factor[None, None]).astype(jnp.bfloat16)
    coef_rows = jnp.moveaxis(coef, 2, 0)
    return lax.map(lambda item: row_synthesis(item[0], item[1]), (coef_rows, row_points))
```

```python
import math

import jax
import jax.numpy as jnp
import numpy as np
from jax import lax
from jax.sharding import Mesh
from jax.sharding import PartitionSpec as P


def angles(remainder, points):
    return 2.0 * math.pi * remainder.astype(jnp.float32) / points.astype(jnp.float32)


def row_synthesis(coef_row, points):
    fields = coef_row.shape[1]
    waves = coef_row.shape[2]
    ablocks = waves // 64
    lon_len = 20 + 4 * (waves - 1)
    lon_idx = jnp.arange(lon_len, dtype=jnp.int32)
    inner = jnp.arange(64, dtype=jnp.int32)
    remainder = inner[:, None] * lon_idx[None, :] % points
    theta = angles(remainder, points)
    cosb = jnp.cos(theta).astype(jnp.bfloat16)
    sinb = jnp.sin(theta).astype(jnp.bfloat16)
    table = jnp.stack([jnp.stack([cosb, sinb], 1), jnp.stack([-sinb, cosb], 1)], 0)
    blocks = coef_row.reshape(2, fields, ablocks, 64)
    part = jnp.einsum("cfab,cbdi->dfai", blocks, table, preferred_element_type=jnp.float32)
    outer = jnp.arange(ablocks, dtype=jnp.int32) * 64
    phase = angles(outer[:, None] * lon_idx[None, :] % points, points)
    total = jnp.sum(part[0] * jnp.cos(phase)[None] - part[1] * jnp.sin(phase)[None], axis=1)
    return jnp.where(lon_idx[None, :] < points, total, jnp.zeros_like(total))


def on_device(spec, legendre, slot_wave, row_lons, band_rows, rows_per_dev):
    n_wave = lax.axis_size("wave")
    n_g = lax.axis_size("lev_g")
    n_r = lax.axis_size("lev_r")
    n_lev = n_g * n_r
    per_dev = legendre.shape[0]
    nlath = legendre.shape[1]
    waves = spec.shape[-1]
    trunc_top = waves - 1
    lev_idx = lax.axis_index("lev_g") * n_r + lax.axis_index("lev_r")
    gathered = lax.all_to_all(spec, ("lev_g", "lev_r"), split_axis=0, concat_axis=2, tiled=True)
    fields = gathered.shape[2]
    first_slot = (lax.axis_index("wave") * n_lev + lev_idx) * per_dev
    my_waves = lax.dynamic_slice_in_dim(slot_wave, first_slot, per_dev)
    degree = jnp.arange(waves, dtype=jnp.int32)
    live_k = degree[None, :] <= trunc_top - my_waves[:, None]
    even_mask = (live_k & (degree[None, :] % 2 == 0))[:, None, :]
    odd_mask = (live_k & (degree[None, :] % 2 == 1))[:, None, :]
    zeros = jnp.zeros_like(legendre)
    leg2 = jnp.concatenate(
        [jnp.where(even_mask, legendre, zeros), jnp.where(odd_mask, legendre, zeros)], 1
    )
    flat = gathered.reshape(per_dev, 2 * fields, waves)
    sums = jnp.einsum("sxk,sjk->sxj", flat, leg2, preferred_element_type=jnp.float32)
    sums = sums.reshape(per_dev, 2, fields, 2, nlath)
    north = band_rows < nlath
    lat_idx = jnp.where(north, band_rows, band_rows - nlath)
    parity_sign = jnp.where(north, 1.0, -1.0).astype(jnp.float32)
    fourier = (sums[:, :, :, 0][..., lat_idx] + parity_sign * sums[:, :, :, 1][..., lat_idx]).astype(
        jnp.bfloat16
    )
    rows = band_rows.shape[0]
    fpg = fields // n_g
    fourier = fourier.reshape(per_dev, 2, n_g, fpg, n_wave, n_r, rows_per_dev)
    fourier = jnp.transpose(fourier, (4, 2, 5, 1, 3, 6, 0))
    fourier = fourier.reshape(n_wave * n_g * n_r, 2, fpg, rows_per_dev, per_dev)
    banded = lax.all_to_all(
        fourier, ("wave", "lev_g", "lev_r"), split_axis=0, concat_axis=0, tiled=True
    )
    banded = jnp.transpose(banded, (1, 2, 3, 0, 4)).reshape(2, fpg, rows_per_dev, -1)
    wave_idx = jnp.arange(waves, dtype=jnp.int32)
    onehot = (slot_wave[:, None] == wave_idx[None, :]).astype(jnp.bfloat16)
    coef = jnp.einsum("cfrs,sm->cfrm", banded, onehot, preferred_element_type=jnp.float32)
    first_row = (lax.axis_index("wave") * n_r + lax.axis_index("lev_r")) * rows_per_dev
    my_rows = lax.dynamic_slice_in_dim(band_rows, first_row, rows_per_dev)
    row_points = row_lons[my_rows]
    keep = 2 * wave_idx[None, :] < row_points[:, None]
    factor = jnp.where(keep, jnp.where(wave_idx[None, :] == 0, 1.0, 2.0), 0.0).astype(jnp.float32)
    coef = (coef * factor[None, None]).astype(jnp.bfloat16)
    coef_rows = jnp.moveaxis(coef, 2, 0)
    if rows_per_dev == 1:
        grid = row_synthesis(coef_rows[0], row_points[0])[None]
    else:
        grid = lax.map(lambda item: row_synthesis(item[0], item[1]), (coef_rows, row_points))
    lon = grid.shape[-1]
    fpd = fpg // n_r
    grid = grid.reshape(rows_per_dev, n_r, fpd, lon)
    grid = lax.all_to_all(grid, "lev_r", split_axis=1, concat_axis=0, tiled=True)
    return grid.reshape(n_r * rows_per_dev, fpd, lon)


def solution(mesh):
    def run(spec, legendre, slot_wave, row_lons, band_rows):
        n_wave = mesh.shape["wave"]
        n_lev = mesh.shape["lev"]
        rows_w = band_rows.shape[0] // n_wave
        if n_lev >= rows_w:
            n_r = rows_w
            rows_per_dev = 1
        else:
            n_r = n_lev
            rows_per_dev = rows_w // n_lev
        n_g = n_lev // n_r
        devs = np.asarray(mesh.devices).reshape(n_wave, n_g, n_r)
        mesh2 = Mesh(devs, ("wave", "lev_g", "lev_r"))
        lev = ("lev_g", "lev_r")
        fn = jax.shard_map(
            lambda *a: on_device(*a, rows_per_dev=rows_per_dev),
            mesh=mesh2,
            in_specs=(P("wave", None, lev, None), P(("wave",) + lev, None, None), P(), P(), P()),
            out_specs=P("wave", lev, None),
            check_vma=False,
        )
        return fn(spec, legendre, slot_wave, row_lons, band_rows)

    return run
```

```python
import math

import jax
import jax.numpy as jnp
import numpy as np
from jax import lax
from jax.sharding import Mesh
from jax.sharding import PartitionSpec as P


def angles(remainder, points):
    return 2.0 * math.pi * remainder.astype(jnp.float32) / points.astype(jnp.float32)


def trig_pair(step, lon_idx, points, count):
    mult = jnp.arange(count, dtype=jnp.int32)[:, None] * step
    theta = angles(mult * lon_idx[None, :] % points, points)
    return jnp.cos(theta), jnp.sin(theta)


def compose(first, second):
    c0, s0 = first
    c1, s1 = second
    cos = c1[:, None] * c0[None] - s1[:, None] * s0[None]
    sin = s1[:, None] * c0[None] + c1[:, None] * s0[None]
    return cos.reshape(-1, cos.shape[-1]), sin.reshape(-1, sin.shape[-1])


def row_synthesis(coef_row, points):
    fields = coef_row.shape[1]
    waves = coef_row.shape[2]
    ablocks = waves // 64
    lon_len = 20 + 4 * (waves - 1)
    lon_idx = jnp.arange(lon_len, dtype=jnp.int32)
    cos_t, sin_t = compose(trig_pair(1, lon_idx, points, 8), trig_pair(8, lon_idx, points, 8))
    cosb = cos_t.astype(jnp.bfloat16)
    sinb = sin_t.astype(jnp.bfloat16)
    n_a1 = -(-ablocks // 4)
    cosp, sinp = compose(
        trig_pair(64, lon_idx, points, 4), trig_pair(256, lon_idx, points, n_a1)
    )
    cosp = cosp[:ablocks]
    sinp = sinp[:ablocks]
    blocks = coef_row.reshape(2, fields, ablocks, 64)
    c0 = blocks[0]
    c1 = blocks[1]
    lhs = jnp.stack(
        [jnp.concatenate([c0, -c1], -1), jnp.concatenate([c1, c0], -1)], 0
    )
    rhs = jnp.concatenate([cosb, sinb], 0)
    part = jnp.einsum("dfab,bi->dfai", lhs, rhs, preferred_element_type=jnp.float32)
    total = jnp.sum(part[0] * cosp[None] - part[1] * sinp[None], axis=1)
    return jnp.where(lon_idx[None, :] < points, total, jnp.zeros_like(total))


def on_device(spec, legendre, slot_wave, row_lons, band_rows, rows_per_dev):
    n_wave = lax.axis_size("wave")
    n_g = lax.axis_size("lev_g")
    n_r = lax.axis_size("lev_r")
    n_lev = n_g * n_r
    per_dev = legendre.shape[0]
    nlath = legendre.shape[1]
    waves = spec.shape[-1]
    trunc_top = waves - 1
    lev_idx = lax.axis_index("lev_g") * n_r + lax.axis_index("lev_r")
    gathered = lax.all_to_all(spec, ("lev_g", "lev_r"), split_axis=0, concat_axis=2, tiled=True)
    fields = gathered.shape[2]
    first_slot = (lax.axis_index("wave") * n_lev + lev_idx) * per_dev
    my_waves = lax.dynamic_slice_in_dim(slot_wave, first_slot, per_dev)
    degree = jnp.arange(waves, dtype=jnp.int32)
    live_k = degree[None, :] <= trunc_top - my_waves[:, None]
    even_mask = (live_k & (degree[None, :] % 2 == 0))[:, None, :]
    odd_mask = (live_k & (degree[None, :] % 2 == 1))[:, None, :]
    zeros = jnp.zeros_like(legendre)
    leg2 = jnp.concatenate(
        [jnp.where(even_mask, legendre, zeros), jnp.where(odd_mask, legendre, zeros)], 1
    )
    flat = gathered.reshape(per_dev, 2 * fields, waves)
    sums = jnp.einsum("sxk,sjk->sxj", flat, leg2, preferred_element_type=jnp.float32)
    sums = sums.reshape(per_dev, 2, fields, 2, nlath)
    north = band_rows < nlath
    lat_idx = jnp.where(north, band_rows, band_rows - nlath)
    parity_sign = jnp.where(north, 1.0, -1.0).astype(jnp.float32)
    fourier = (sums[:, :, :, 0][..., lat_idx] + parity_sign * sums[:, :, :, 1][..., lat_idx]).astype(
        jnp.bfloat16
    )
    rows = band_rows.shape[0]
    fpg = fields // n_g
    fourier = fourier.reshape(per_dev, 2, n_g, fpg, n_wave, n_r, rows_per_dev)
    fourier = jnp.transpose(fourier, (4, 2, 5, 1, 3, 6, 0))
    fourier = fourier.reshape(n_wave * n_g * n_r, 2, fpg, rows_per_dev, per_dev)
    banded = lax.all_to_all(
        fourier, ("wave", "lev_g", "lev_r"), split_axis=0, concat_axis=0, tiled=True
    )
    banded = jnp.transpose(banded, (1, 2, 3, 0, 4)).reshape(2, fpg, rows_per_dev, -1)
    wave_idx = jnp.arange(waves, dtype=jnp.int32)
    onehot = (slot_wave[:, None] == wave_idx[None, :]).astype(jnp.bfloat16)
    coef = jnp.einsum("cfrs,sm->cfrm", banded, onehot, preferred_element_type=jnp.float32)
    first_row = (lax.axis_index("wave") * n_r + lax.axis_index("lev_r")) * rows_per_dev
    my_rows = lax.dynamic_slice_in_dim(band_rows, first_row, rows_per_dev)
    row_points = row_lons[my_rows]
    keep = 2 * wave_idx[None, :] < row_points[:, None]
    factor = jnp.where(keep, jnp.where(wave_idx[None, :] == 0, 1.0, 2.0), 0.0).astype(jnp.float32)
    coef = (coef * factor[None, None]).astype(jnp.bfloat16)
    coef_rows = jnp.moveaxis(coef, 2, 0)
    if rows_per_dev == 1:
        grid = row_synthesis(coef_rows[0], row_points[0])[None]
    else:
        grid = lax.map(lambda item: row_synthesis(item[0], item[1]), (coef_rows, row_points))
    lon = grid.shape[-1]
    fpd = fpg // n_r
    grid = grid.reshape(rows_per_dev, n_r, fpd, lon)
    grid = lax.all_to_all(grid, "lev_r", split_axis=1, concat_axis=0, tiled=True)
    return grid.reshape(n_r * rows_per_dev, fpd, lon)


def solution(mesh):
    def run(spec, legendre, slot_wave, row_lons, band_rows):
        n_wave = mesh.shape["wave"]
        n_lev = mesh.shape["lev"]
        rows_w = band_rows.shape[0] // n_wave
        if n_lev >= rows_w:
            n_r = rows_w
            rows_per_dev = 1
        else:
            n_r = n_lev
            rows_per_dev = rows_w // n_lev
        n_g = n_lev // n_r
        devs = np.asarray(mesh.devices).reshape(n_wave, n_g, n_r)
        mesh2 = Mesh(devs, ("wave", "lev_g", "lev_r"))
        lev = ("lev_g", "lev_r")
        fn = jax.shard_map(
            lambda *a: on_device(*a, rows_per_dev=rows_per_dev),
            mesh=mesh2,
            in_specs=(P("wave", None, lev, None), P(("wave",) + lev, None, None), P(), P(), P()),
            out_specs=P("wave", lev, None),
            check_vma=False,
        )
        return fn(spec, legendre, slot_wave, row_lons, band_rows)

    return run
```

```python
import math

import jax
import jax.numpy as jnp
import numpy as np
from jax import lax
from jax.sharding import Mesh
from jax.sharding import PartitionSpec as P


def angles(remainder, points):
    return 2.0 * math.pi * remainder.astype(jnp.float32) / points.astype(jnp.float32)


def trig_pair(step, lon_idx, points, count):
    mult = jnp.arange(count, dtype=jnp.int32)[:, None] * step
    theta = angles(mult * lon_idx[None, :] % points, points)
    return jnp.cos(theta), jnp.sin(theta)


def compose(first, second):
    c0, s0 = first
    c1, s1 = second
    cos = c1[:, None] * c0[None] - s1[:, None] * s0[None]
    sin = s1[:, None] * c0[None] + c1[:, None] * s0[None]
    return cos.reshape(-1, cos.shape[-1]), sin.reshape(-1, sin.shape[-1])


def row_synthesis(coef_row, points):
    fields = coef_row.shape[1]
    waves = coef_row.shape[2]
    ablocks = waves // 64
    lon_len = 20 + 4 * (waves - 1)
    lon_idx = jnp.arange(lon_len, dtype=jnp.int32)
    cos_t, sin_t = compose(trig_pair(1, lon_idx, points, 8), trig_pair(8, lon_idx, points, 8))
    cosb = cos_t.astype(jnp.bfloat16)
    sinb = sin_t.astype(jnp.bfloat16)
    n_a1 = -(-ablocks // 4)
    cosp, sinp = compose(
        trig_pair(64, lon_idx, points, 4), trig_pair(256, lon_idx, points, n_a1)
    )
    cosp = cosp[:ablocks]
    sinp = sinp[:ablocks]
    blocks = coef_row.reshape(2, fields, ablocks, 64)
    c0 = blocks[0]
    c1 = blocks[1]
    lhs = jnp.stack(
        [jnp.concatenate([c0, -c1], -1), jnp.concatenate([c1, c0], -1)], 0
    )
    rhs = jnp.concatenate([cosb, sinb], 0)
    part = jnp.einsum("dfab,bi->dfai", lhs, rhs, preferred_element_type=jnp.float32)
    total = jnp.sum(part[0] * cosp[None] - part[1] * sinp[None], axis=1)
    return jnp.where(lon_idx[None, :] < points, total, jnp.zeros_like(total))


def on_device(spec, legendre, slot_wave, row_lons, band_rows, rows_per_dev):
    n_wave = lax.axis_size("wave")
    n_g = lax.axis_size("lev_g")
    n_r = lax.axis_size("lev_r")
    n_lev = n_g * n_r
    per_dev = legendre.shape[0]
    nlath = legendre.shape[1]
    waves = spec.shape[-1]
    trunc_top = waves - 1
    lev_idx = lax.axis_index("lev_g") * n_r + lax.axis_index("lev_r")
    spec_v = spec.reshape((n_lev, per_dev) + spec.shape[1:])
    gathered = lax.all_to_all(spec_v, ("lev_g", "lev_r"), split_axis=0, concat_axis=0, tiled=True)
    fields = gathered.shape[3] * n_lev
    first_slot = (lax.axis_index("wave") * n_lev + lev_idx) * per_dev
    my_waves = lax.dynamic_slice_in_dim(slot_wave, first_slot, per_dev)
    degree = jnp.arange(waves, dtype=jnp.int32)
    live_k = degree[None, :] <= trunc_top - my_waves[:, None]
    even_mask = (live_k & (degree[None, :] % 2 == 0))[:, None, :]
    odd_mask = (live_k & (degree[None, :] % 2 == 1))[:, None, :]
    zeros = jnp.zeros_like(legendre)
    leg2 = jnp.concatenate(
        [jnp.where(even_mask, legendre, zeros), jnp.where(odd_mask, legendre, zeros)], 1
    )
    sums = jnp.einsum("lscfk,sjk->sclfj", gathered, leg2, preferred_element_type=jnp.float32)
    sums = sums.reshape(per_dev, 2, fields, 2, nlath)
    north = band_rows < nlath
    lat_idx = jnp.where(north, band_rows, band_rows - nlath)
    parity_sign = jnp.where(north, 1.0, -1.0).astype(jnp.float32)
    fourier = (sums[:, :, :, 0][..., lat_idx] + parity_sign * sums[:, :, :, 1][..., lat_idx]).astype(
        jnp.bfloat16
    )
    rows = band_rows.shape[0]
    fpg = fields // n_g
    fourier = fourier.reshape(per_dev, 2, n_g, fpg, n_wave, n_r, rows_per_dev)
    fourier = jnp.transpose(fourier, (4, 2, 5, 1, 3, 6, 0))
    fourier = fourier.reshape(n_wave * n_g * n_r, 2, fpg, rows_per_dev, per_dev)
    banded = lax.all_to_all(
        fourier, ("wave", "lev_g", "lev_r"), split_axis=0, concat_axis=0, tiled=True
    )
    banded = jnp.transpose(banded, (1, 2, 3, 0, 4)).reshape(2, fpg, rows_per_dev, -1)
    wave_idx = jnp.arange(waves, dtype=jnp.int32)
    onehot = (slot_wave[:, None] == wave_idx[None, :]).astype(jnp.bfloat16)
    coef = jnp.einsum("cfrs,sm->cfrm", banded, onehot, preferred_element_type=jnp.float32)
    first_row = (lax.axis_index("wave") * n_r + lax.axis_index("lev_r")) * rows_per_dev
    my_rows = lax.dynamic_slice_in_dim(band_rows, first_row, rows_per_dev)
    row_points = row_lons[my_rows]
    keep = 2 * wave_idx[None, :] < row_points[:, None]
    factor = jnp.where(keep, jnp.where(wave_idx[None, :] == 0, 1.0, 2.0), 0.0).astype(jnp.float32)
    coef = (coef * factor[None, None]).astype(jnp.bfloat16)
    coef_rows = jnp.moveaxis(coef, 2, 0)
    if rows_per_dev == 1:
        grid = row_synthesis(coef_rows[0], row_points[0])[None]
    else:
        grid = lax.map(lambda item: row_synthesis(item[0], item[1]), (coef_rows, row_points))
    lon = grid.shape[-1]
    fpd = fpg // n_r
    grid = grid.reshape(rows_per_dev, n_r, fpd, lon)
    grid = lax.all_to_all(grid, "lev_r", split_axis=1, concat_axis=0, tiled=True)
    return grid.reshape(n_r * rows_per_dev, fpd, lon)


def solution(mesh):
    def run(spec, legendre, slot_wave, row_lons, band_rows):
        n_wave = mesh.shape["wave"]
        n_lev = mesh.shape["lev"]
        rows_w = band_rows.shape[0] // n_wave
        if n_lev >= rows_w:
            n_r = rows_w
            rows_per_dev = 1
        else:
            n_r = n_lev
            rows_per_dev = rows_w // n_lev
        n_g = n_lev // n_r
        devs = np.asarray(mesh.devices).reshape(n_wave, n_g, n_r)
        mesh2 = Mesh(devs, ("wave", "lev_g", "lev_r"))
        lev = ("lev_g", "lev_r")
        fn = jax.shard_map(
            lambda *a: on_device(*a, rows_per_dev=rows_per_dev),
            mesh=mesh2,
            in_specs=(P("wave", None, lev, None), P(("wave",) + lev, None, None), P(), P(), P()),
            out_specs=P("wave", lev, None),
            check_vma=False,
        )
        return fn(spec, legendre, slot_wave, row_lons, band_rows)

    return run
```

```python
import math

import jax
import jax.numpy as jnp
import numpy as np
from jax import lax
from jax.sharding import Mesh
from jax.sharding import PartitionSpec as P


def angles(remainder, points):
    return 2.0 * math.pi * remainder.astype(jnp.float32) / points.astype(jnp.float32)


def trig_pair(step, lon_idx, points, count):
    mult = jnp.arange(count, dtype=jnp.int32)[:, None] * step
    theta = angles(mult * lon_idx[None, :] % points, points)
    return jnp.cos(theta), jnp.sin(theta)


def compose(first, second):
    c0, s0 = first
    c1, s1 = second
    cos = c1[:, None] * c0[None] - s1[:, None] * s0[None]
    sin = s1[:, None] * c0[None] + c1[:, None] * s0[None]
    return cos.reshape(-1, cos.shape[-1]), sin.reshape(-1, sin.shape[-1])


def row_synthesis(coef_row, points):
    fields = coef_row.shape[1]
    waves = coef_row.shape[2]
    ablocks = waves // 64
    lon_len = 20 + 4 * (waves - 1)
    lon_idx = jnp.arange(lon_len, dtype=jnp.int32)
    cos_t, sin_t = compose(trig_pair(1, lon_idx, points, 8), trig_pair(8, lon_idx, points, 8))
    cosb = cos_t.astype(jnp.bfloat16)
    sinb = sin_t.astype(jnp.bfloat16)
    n_a1 = -(-ablocks // 4)
    cosp, sinp = compose(
        trig_pair(64, lon_idx, points, 4), trig_pair(256, lon_idx, points, n_a1)
    )
    cosp = cosp[:ablocks]
    sinp = sinp[:ablocks]
    blocks = coef_row.reshape(2, fields, ablocks, 64)
    c0 = blocks[0]
    c1 = blocks[1]
    lhs = jnp.stack(
        [jnp.concatenate([c0, -c1], -1), jnp.concatenate([c1, c0], -1)], 0
    )
    rhs = jnp.concatenate([cosb, sinb], 0)
    part = jnp.einsum("dfab,bi->dfai", lhs, rhs, preferred_element_type=jnp.float32)
    total = jnp.sum(part[0] * cosp[None] - part[1] * sinp[None], axis=1)
    return jnp.where(lon_idx[None, :] < points, total, jnp.zeros_like(total))


def on_device(spec, legendre, slot_wave, row_lons, band_rows, rows_per_dev):
    n_wave = lax.axis_size("wave")
    n_g = lax.axis_size("lev_g")
    n_r = lax.axis_size("lev_r")
    n_lev = n_g * n_r
    per_dev = legendre.shape[0]
    nlath = legendre.shape[1]
    waves = spec.shape[-1]
    trunc_top = waves - 1
    lev_idx = lax.axis_index("lev_g") * n_r + lax.axis_index("lev_r")
    fpd = spec.shape[2]
    spec_v = spec.reshape(n_lev, per_dev * 2 * fpd, waves)
    gathered = lax.all_to_all(spec_v, ("lev_g", "lev_r"), split_axis=0, concat_axis=0, tiled=True)
    gathered = gathered.reshape(n_lev, per_dev, 2, fpd, waves)
    fields = fpd * n_lev
    first_slot = (lax.axis_index("wave") * n_lev + lev_idx) * per_dev
    my_waves = lax.dynamic_slice_in_dim(slot_wave, first_slot, per_dev)
    degree = jnp.arange(waves, dtype=jnp.int32)
    live_k = degree[None, :] <= trunc_top - my_waves[:, None]
    even_mask = (live_k & (degree[None, :] % 2 == 0))[:, None, :]
    odd_mask = (live_k & (degree[None, :] % 2 == 1))[:, None, :]
    zeros = jnp.zeros_like(legendre)
    leg2 = jnp.concatenate(
        [jnp.where(even_mask, legendre, zeros), jnp.where(odd_mask, legendre, zeros)], 1
    )
    sums = jnp.einsum("lscfk,sjk->sclfj", gathered, leg2, preferred_element_type=jnp.float32)
    sums = sums.reshape(per_dev, 2, fields, 2, nlath)
    north = band_rows < nlath
    lat_idx = jnp.where(north, band_rows, band_rows - nlath)
    parity_sign = jnp.where(north, 1.0, -1.0).astype(jnp.float32)
    fourier = (sums[:, :, :, 0][..., lat_idx] + parity_sign * sums[:, :, :, 1][..., lat_idx]).astype(
        jnp.bfloat16
    )
    rows = band_rows.shape[0]
    fpg = fields // n_g
    fourier = fourier.reshape(per_dev, 2, n_g, fpg, n_wave, n_r, rows_per_dev)
    fourier = jnp.transpose(fourier, (4, 2, 5, 1, 3, 6, 0))
    fourier = fourier.reshape(n_wave * n_g * n_r, 2, fpg, rows_per_dev, per_dev)
    banded = lax.all_to_all(
        fourier, ("wave", "lev_g", "lev_r"), split_axis=0, concat_axis=0, tiled=True
    )
    banded = jnp.transpose(banded, (1, 2, 3, 0, 4)).reshape(2, fpg, rows_per_dev, -1)
    wave_idx = jnp.arange(waves, dtype=jnp.int32)
    onehot = (slot_wave[:, None] == wave_idx[None, :]).astype(jnp.bfloat16)
    coef = jnp.einsum("cfrs,sm->cfrm", banded, onehot, preferred_element_type=jnp.float32)
    first_row = (lax.axis_index("wave") * n_r + lax.axis_index("lev_r")) * rows_per_dev
    my_rows = lax.dynamic_slice_in_dim(band_rows, first_row, rows_per_dev)
    row_points = row_lons[my_rows]
    keep = 2 * wave_idx[None, :] < row_points[:, None]
    factor = jnp.where(keep, jnp.where(wave_idx[None, :] == 0, 1.0, 2.0), 0.0).astype(jnp.float32)
    coef = (coef * factor[None, None]).astype(jnp.bfloat16)
    coef_rows = jnp.moveaxis(coef, 2, 0)
    if rows_per_dev == 1:
        grid = row_synthesis(coef_rows[0], row_points[0])[None]
    else:
        grid = lax.map(lambda item: row_synthesis(item[0], item[1]), (coef_rows, row_points))
    lon = grid.shape[-1]
    fpd = fpg // n_r
    grid = grid.reshape(rows_per_dev, n_r, fpd, lon)
    grid = lax.all_to_all(grid, "lev_r", split_axis=1, concat_axis=0, tiled=True)
    return grid.reshape(n_r * rows_per_dev, fpd, lon)


def solution(mesh):
    def run(spec, legendre, slot_wave, row_lons, band_rows):
        n_wave = mesh.shape["wave"]
        n_lev = mesh.shape["lev"]
        rows_w = band_rows.shape[0] // n_wave
        if n_lev >= rows_w:
            n_r = rows_w
            rows_per_dev = 1
        else:
            n_r = n_lev
            rows_per_dev = rows_w // n_lev
        n_g = n_lev // n_r
        devs = np.asarray(mesh.devices).reshape(n_wave, n_g, n_r)
        mesh2 = Mesh(devs, ("wave", "lev_g", "lev_r"))
        lev = ("lev_g", "lev_r")
        fn = jax.shard_map(
            lambda *a: on_device(*a, rows_per_dev=rows_per_dev),
            mesh=mesh2,
            in_specs=(P("wave", None, lev, None), P(("wave",) + lev, None, None), P(), P(), P()),
            out_specs=P("wave", lev, None),
            check_vma=False,
        )
        return fn(spec, legendre, slot_wave, row_lons, band_rows)

    return run
```

```python
import math

import jax
import jax.numpy as jnp
import numpy as np
from jax import lax
from jax.sharding import Mesh
from jax.sharding import PartitionSpec as P


def angles(remainder, points):
    return 2.0 * math.pi * remainder.astype(jnp.float32) / points.astype(jnp.float32)


def cmul(x, y):
    return x[0] * y[0] - x[1] * y[1], x[0] * y[1] + x[1] * y[0]


def powers(base, count):
    out = [(jnp.ones_like(base[0]), jnp.zeros_like(base[1])), base]
    while len(out) < count:
        out.append(cmul(out[-1], base))
    out = out[:count]
    return jnp.stack([o[0] for o in out], 1), jnp.stack([o[1] for o in out], 1)


def outer(first, second):
    c0, s0 = first
    c1, s1 = second
    cos = c1[:, :, None] * c0[:, None] - s1[:, :, None] * s0[:, None]
    sin = s1[:, :, None] * c0[:, None] + c1[:, :, None] * s0[:, None]
    shape = (cos.shape[0], -1, cos.shape[-1])
    return cos.reshape(shape), sin.reshape(shape)


def rows_tables(points, waves):
    ablocks = waves // 64
    lon_len = 20 + 4 * (waves - 1)
    lon_idx = jnp.arange(lon_len, dtype=jnp.int32)
    pts = points[:, None]
    steps = jnp.array([1, 64], dtype=jnp.int32)[:, None, None]
    theta = angles(steps * lon_idx[None, None, :] % pts[None], pts[None])
    dc, ds = lax.optimization_barrier((jnp.cos(theta), jnp.sin(theta)))
    e1 = (dc[0], ds[0])
    e64 = (dc[1], ds[1])
    lo = powers(e1, 8)
    e8 = cmul((lo[0][:, 7], lo[1][:, 7]), e1)
    hi = powers(e8, 8)
    cos_t, sin_t = outer(lo, hi)
    rhs = jnp.concatenate([cos_t.astype(jnp.bfloat16), sin_t.astype(jnp.bfloat16)], 1)
    p0 = powers(e64, 4)
    e256 = cmul((p0[0][:, 3], p0[1][:, 3]), e64)
    n_a1 = -(-ablocks // 4)
    p1 = powers(e256, n_a1)
    return rhs, p0, p1


def row_synthesis(coef_row, rhs, p0c, p0s, p1c, p1s, points):
    fields = coef_row.shape[1]
    waves = coef_row.shape[2]
    ablocks = waves // 64
    lon_idx = jnp.arange(rhs.shape[-1], dtype=jnp.int32)
    cosp, sinp = outer((p0c[None], p0s[None]), (p1c[None], p1s[None]))
    cosp = cosp[0, :ablocks]
    sinp = sinp[0, :ablocks]
    blocks = coef_row.reshape(2, fields, ablocks, 64)
    c0 = blocks[0]
    c1 = blocks[1]
    lhs = jnp.stack(
        [jnp.concatenate([c0, -c1], -1), jnp.concatenate([c1, c0], -1)], 0
    )
    part = jnp.einsum("dfab,bi->dfai", lhs, rhs, preferred_element_type=jnp.float32)
    total = jnp.sum(part[0] * cosp[None] - part[1] * sinp[None], axis=1)
    return jnp.where(lon_idx[None, :] < points, total, jnp.zeros_like(total))


def on_device(spec, legendre, slot_wave, row_lons, band_rows, rows_per_dev):
    n_wave = lax.axis_size("wave")
    n_g = lax.axis_size("lev_g")
    n_r = lax.axis_size("lev_r")
    n_lev = n_g * n_r
    per_dev = legendre.shape[0]
    nlath = legendre.shape[1]
    waves = spec.shape[-1]
    trunc_top = waves - 1
    lev_idx = lax.axis_index("lev_g") * n_r + lax.axis_index("lev_r")
    spec_v = spec.reshape((n_lev, per_dev) + spec.shape[1:])
    gathered = lax.all_to_all(spec_v, ("lev_g", "lev_r"), split_axis=0, concat_axis=0, tiled=True)
    fields = gathered.shape[3] * n_lev
    first_row = (lax.axis_index("wave") * n_r + lax.axis_index("lev_r")) * rows_per_dev
    my_rows = lax.dynamic_slice_in_dim(band_rows, first_row, rows_per_dev)
    row_points = row_lons[my_rows]
    rhs_all, p0_all, p1_all = rows_tables(row_points, waves)
    first_slot = (lax.axis_index("wave") * n_lev + lev_idx) * per_dev
    my_waves = lax.dynamic_slice_in_dim(slot_wave, first_slot, per_dev)
    degree = jnp.arange(waves, dtype=jnp.int32)
    live_k = degree[None, :] <= trunc_top - my_waves[:, None]
    even_mask = (live_k & (degree[None, :] % 2 == 0))[:, None, :]
    odd_mask = (live_k & (degree[None, :] % 2 == 1))[:, None, :]
    zeros = jnp.zeros_like(legendre)
    leg2 = jnp.concatenate(
        [jnp.where(even_mask, legendre, zeros), jnp.where(odd_mask, legendre, zeros)], 1
    )
    sums = jnp.einsum("lscfk,sjk->sclfj", gathered, leg2, preferred_element_type=jnp.float32)
    sums = sums.reshape(per_dev, 2, fields, 2, nlath)
    north = band_rows < nlath
    lat_idx = jnp.where(north, band_rows, band_rows - nlath)
    parity_sign = jnp.where(north, 1.0, -1.0).astype(jnp.float32)
    fourier = (sums[:, :, :, 0][..., lat_idx] + parity_sign * sums[:, :, :, 1][..., lat_idx]).astype(
        jnp.bfloat16
    )
    rows = band_rows.shape[0]
    fpg = fields // n_g
    fourier = fourier.reshape(per_dev, 2, n_g, fpg, n_wave, n_r, rows_per_dev)
    fourier = jnp.transpose(fourier, (4, 2, 5, 1, 3, 6, 0))
    fourier = fourier.reshape(n_wave * n_g * n_r, 2, fpg, rows_per_dev, per_dev)
    banded = lax.all_to_all(
        fourier, ("wave", "lev_g", "lev_r"), split_axis=0, concat_axis=0, tiled=True
    )
    banded = jnp.transpose(banded, (1, 2, 3, 0, 4)).reshape(2, fpg, rows_per_dev, -1)
    wave_idx = jnp.arange(waves, dtype=jnp.int32)
    onehot = (slot_wave[:, None] == wave_idx[None, :]).astype(jnp.bfloat16)
    coef = jnp.einsum("cfrs,sm->cfrm", banded, onehot, preferred_element_type=jnp.float32)
    keep = 2 * wave_idx[None, :] < row_points[:, None]
    factor = jnp.where(keep, jnp.where(wave_idx[None, :] == 0, 1.0, 2.0), 0.0).astype(jnp.float32)
    coef = (coef * factor[None, None]).astype(jnp.bfloat16)
    coef_rows = jnp.moveaxis(coef, 2, 0)
    grid = lax.map(
        lambda item: row_synthesis(*item), (coef_rows, rhs_all, p0_all[0], p0_all[1], p1_all[0], p1_all[1], row_points)
    )
    lon = grid.shape[-1]
    fpd = fpg // n_r
    grid = grid.reshape(rows_per_dev, n_r, fpd, lon)
    grid = lax.all_to_all(grid, "lev_r", split_axis=1, concat_axis=0, tiled=True)
    return grid.reshape(n_r * rows_per_dev, fpd, lon)


def solution(mesh):
    def run(spec, legendre, slot_wave, row_lons, band_rows):
        n_wave = mesh.shape["wave"]
        n_lev = mesh.shape["lev"]
        rows_w = band_rows.shape[0] // n_wave
        n_r = 1
        rows_per_dev = rows_w
        n_g = n_lev // n_r
        devs = np.asarray(mesh.devices).reshape(n_wave, n_g, n_r)
        mesh2 = Mesh(devs, ("wave", "lev_g", "lev_r"))
        lev = ("lev_g", "lev_r")
        fn = jax.shard_map(
            lambda *a: on_device(*a, rows_per_dev=rows_per_dev),
            mesh=mesh2,
            in_specs=(P("wave", None, lev, None), P(("wave",) + lev, None, None), P(), P(), P()),
            out_specs=P("wave", lev, None),
            check_vma=False,
        )
        return fn(spec, legendre, slot_wave, row_lons, band_rows)

    return run
```

```python
import math

import jax
import jax.numpy as jnp
import numpy as np
from jax import lax
from jax.sharding import Mesh
from jax.sharding import PartitionSpec as P


def angles(remainder, points):
    return 2.0 * math.pi * remainder.astype(jnp.float32) / points.astype(jnp.float32)


def trig_pair(step, lon_idx, points, count):
    mult = jnp.arange(count, dtype=jnp.int32)[:, None] * step
    theta = angles(mult * lon_idx[None, :] % points, points)
    return jnp.cos(theta), jnp.sin(theta)


def compose(first, second):
    c0, s0 = first
    c1, s1 = second
    cos = c1[:, None] * c0[None] - s1[:, None] * s0[None]
    sin = s1[:, None] * c0[None] + c1[:, None] * s0[None]
    return cos.reshape(-1, cos.shape[-1]), sin.reshape(-1, sin.shape[-1])


def row_tables(points, waves):
    ablocks = waves // 64
    lon_len = 20 + 4 * (waves - 1)
    lon_idx = jnp.arange(lon_len, dtype=jnp.int32)
    cos_t, sin_t = compose(trig_pair(1, lon_idx, points, 8), trig_pair(8, lon_idx, points, 8))
    rhs = jnp.concatenate([cos_t.astype(jnp.bfloat16), sin_t.astype(jnp.bfloat16)], 0)
    n_a1 = -(-ablocks // 4)
    cosp, sinp = compose(
        trig_pair(64, lon_idx, points, 4), trig_pair(256, lon_idx, points, n_a1)
    )
    return rhs, cosp[:ablocks], sinp[:ablocks]


def row_synthesis(coef_row, rhs, cosp, sinp, points):
    fields = coef_row.shape[1]
    waves = coef_row.shape[2]
    ablocks = waves // 64
    lon_idx = jnp.arange(rhs.shape[-1], dtype=jnp.int32)
    blocks = coef_row.reshape(2, fields, ablocks, 64)
    c0 = blocks[0]
    c1 = blocks[1]
    lhs = jnp.stack(
        [jnp.concatenate([c0, -c1], -1), jnp.concatenate([c1, c0], -1)], 0
    )
    part = jnp.einsum("dfab,bi->dfai", lhs, rhs, preferred_element_type=jnp.float32)
    total = jnp.sum(part[0] * cosp[None] - part[1] * sinp[None], axis=1)
    return jnp.where(lon_idx[None, :] < points, total, jnp.zeros_like(total))


def on_device(spec, legendre, slot_wave, row_lons, band_rows, rows_per_dev):
    n_wave = lax.axis_size("wave")
    n_g = lax.axis_size("lev_g")
    n_r = lax.axis_size("lev_r")
    n_lev = n_g * n_r
    per_dev = legendre.shape[0]
    nlath = legendre.shape[1]
    waves = spec.shape[-1]
    trunc_top = waves - 1
    lev_idx = lax.axis_index("lev_g") * n_r + lax.axis_index("lev_r")
    spec_v = spec.reshape((n_lev, per_dev) + spec.shape[1:])
    gathered = lax.all_to_all(spec_v, ("lev_g", "lev_r"), split_axis=0, concat_axis=0, tiled=True)
    fields = gathered.shape[3] * n_lev
    first_row = (lax.axis_index("wave") * n_r + lax.axis_index("lev_r")) * rows_per_dev
    my_rows = lax.dynamic_slice_in_dim(band_rows, first_row, rows_per_dev)
    row_points = row_lons[my_rows]
    if rows_per_dev == 1:
        tables = tuple(t[None] for t in row_tables(row_points[0], waves))
    else:
        tables = lax.map(lambda p: row_tables(p, waves), row_points)
    gathered, tables = lax.optimization_barrier((gathered, tables))
    first_slot = (lax.axis_index("wave") * n_lev + lev_idx) * per_dev
    my_waves = lax.dynamic_slice_in_dim(slot_wave, first_slot, per_dev)
    degree = jnp.arange(waves, dtype=jnp.int32)
    live_k = degree[None, :] <= trunc_top - my_waves[:, None]
    even_mask = (live_k & (degree[None, :] % 2 == 0))[:, None, :]
    odd_mask = (live_k & (degree[None, :] % 2 == 1))[:, None, :]
    zeros = jnp.zeros_like(legendre)
    leg2 = jnp.concatenate(
        [jnp.where(even_mask, legendre, zeros), jnp.where(odd_mask, legendre, zeros)], 1
    )
    sums = jnp.einsum("lscfk,sjk->sclfj", gathered, leg2, preferred_element_type=jnp.float32)
    sums = sums.reshape(per_dev, 2, fields, 2, nlath)
    north = band_rows < nlath
    lat_idx = jnp.where(north, band_rows, band_rows - nlath)
    parity_sign = jnp.where(north, 1.0, -1.0).astype(jnp.float32)
    fourier = (sums[:, :, :, 0][..., lat_idx] + parity_sign * sums[:, :, :, 1][..., lat_idx]).astype(
        jnp.bfloat16
    )
    rows = band_rows.shape[0]
    fpg = fields // n_g
    fourier = fourier.reshape(per_dev, 2, n_g, fpg, n_wave, n_r, rows_per_dev)
    fourier = jnp.transpose(fourier, (4, 2, 5, 1, 3, 6, 0))
    fourier = fourier.reshape(n_wave * n_g * n_r, 2, fpg, rows_per_dev, per_dev)
    banded = lax.all_to_all(
        fourier, ("wave", "lev_g", "lev_r"), split_axis=0, concat_axis=0, tiled=True
    )
    banded = jnp.transpose(banded, (1, 2, 3, 0, 4)).reshape(2, fpg, rows_per_dev, -1)
    wave_idx = jnp.arange(waves, dtype=jnp.int32)
    onehot = (slot_wave[:, None] == wave_idx[None, :]).astype(jnp.bfloat16)
    coef = jnp.einsum("cfrs,sm->cfrm", banded, onehot, preferred_element_type=jnp.float32)
    keep = 2 * wave_idx[None, :] < row_points[:, None]
    factor = jnp.where(keep, jnp.where(wave_idx[None, :] == 0, 1.0, 2.0), 0.0).astype(jnp.float32)
    coef = (coef * factor[None, None]).astype(jnp.bfloat16)
    coef_rows = jnp.moveaxis(coef, 2, 0)
    if rows_per_dev == 1:
        grid = row_synthesis(coef_rows[0], *(t[0] for t in tables), row_points[0])[None]
    else:
        grid = lax.map(lambda item: row_synthesis(*item), (coef_rows,) + tuple(tables) + (row_points,))
    lon = grid.shape[-1]
    fpd = fpg // n_r
    grid = grid.reshape(rows_per_dev, n_r, fpd, lon)
    grid = lax.all_to_all(grid, "lev_r", split_axis=1, concat_axis=0, tiled=True)
    return grid.reshape(n_r * rows_per_dev, fpd, lon)


def solution(mesh):
    def run(spec, legendre, slot_wave, row_lons, band_rows):
        n_wave = mesh.shape["wave"]
        n_lev = mesh.shape["lev"]
        rows_w = band_rows.shape[0] // n_wave
        if n_lev >= rows_w:
            n_r = rows_w
            rows_per_dev = 1
        else:
            n_r = n_lev
            rows_per_dev = rows_w // n_lev
        n_g = n_lev // n_r
        devs = np.asarray(mesh.devices).reshape(n_wave, n_g, n_r)
        mesh2 = Mesh(devs, ("wave", "lev_g", "lev_r"))
        lev = ("lev_g", "lev_r")
        fn = jax.shard_map(
            lambda *a: on_device(*a, rows_per_dev=rows_per_dev),
            mesh=mesh2,
            in_specs=(P("wave", None, lev, None), P(("wave",) + lev, None, None), P(), P(), P()),
            out_specs=P("wave", lev, None),
            check_vma=False,
        )
        return fn(spec, legendre, slot_wave, row_lons, band_rows)

    return run
```

```python
import math

import jax
import jax.numpy as jnp
import numpy as np
from jax import lax
from jax.sharding import Mesh
from jax.sharding import PartitionSpec as P


def angles(remainder, points):
    return 2.0 * math.pi * remainder.astype(jnp.float32) / points.astype(jnp.float32)


def trig_pair(step, lon_idx, points, count):
    mult = jnp.arange(count, dtype=jnp.int32)[:, None] * step
    theta = angles(mult * lon_idx[None, :] % points, points)
    return jnp.cos(theta), jnp.sin(theta)


def compose(first, second):
    c0, s0 = first
    c1, s1 = second
    cos = c1[:, None] * c0[None] - s1[:, None] * s0[None]
    sin = s1[:, None] * c0[None] + c1[:, None] * s0[None]
    return cos.reshape(-1, cos.shape[-1]), sin.reshape(-1, sin.shape[-1])


def row_tables(points, waves):
    ablocks = waves // 64
    lon_len = 20 + 4 * (waves - 1)
    lon_idx = jnp.arange(lon_len, dtype=jnp.int32)
    cos_t, sin_t = compose(trig_pair(1, lon_idx, points, 8), trig_pair(8, lon_idx, points, 8))
    rhs = jnp.concatenate([cos_t.astype(jnp.bfloat16), sin_t.astype(jnp.bfloat16)], 0)
    n_a1 = -(-ablocks // 4)
    cosp, sinp = compose(
        trig_pair(64, lon_idx, points, 4), trig_pair(256, lon_idx, points, n_a1)
    )
    return rhs, cosp[:ablocks], sinp[:ablocks]


def row_synthesis(coef_row, rhs, cosp, sinp, points):
    fields = coef_row.shape[1]
    waves = coef_row.shape[2]
    ablocks = waves // 64
    lon_idx = jnp.arange(rhs.shape[-1], dtype=jnp.int32)
    blocks = coef_row.reshape(2, fields, ablocks, 64)
    c0 = blocks[0]
    c1 = blocks[1]
    lhs = jnp.stack(
        [jnp.concatenate([c0, -c1], -1), jnp.concatenate([c1, c0], -1)], 0
    )
    part = jnp.einsum("dfab,bi->dfai", lhs, rhs, preferred_element_type=jnp.float32)
    total = jnp.sum(part[0] * cosp[None] - part[1] * sinp[None], axis=1)
    return jnp.where(lon_idx[None, :] < points, total, jnp.zeros_like(total))


def on_device(spec, legendre, slot_wave, row_lons, band_rows, rows_per_dev):
    n_wave = lax.axis_size("wave")
    n_g = lax.axis_size("lev_g")
    n_r = lax.axis_size("lev_r")
    n_lev = n_g * n_r
    per_dev = legendre.shape[0]
    nlath = legendre.shape[1]
    waves = spec.shape[-1]
    trunc_top = waves - 1
    lev_idx = lax.axis_index("lev_g") * n_r + lax.axis_index("lev_r")
    spec_v = spec.reshape((n_lev, per_dev) + spec.shape[1:])
    gathered = lax.all_to_all(spec_v, ("lev_g", "lev_r"), split_axis=0, concat_axis=0, tiled=True)
    fields = gathered.shape[3] * n_lev
    first_row = (lax.axis_index("wave") * n_r + lax.axis_index("lev_r")) * rows_per_dev
    my_rows = lax.dynamic_slice_in_dim(band_rows, first_row, rows_per_dev)
    row_points = row_lons[my_rows]
    if rows_per_dev == 1:
        tables = tuple(t[None] for t in row_tables(row_points[0], waves))
    else:
        tables = lax.map(lambda p: row_tables(p, waves), row_points)
    gathered, tables = lax.optimization_barrier((gathered, tables))
    first_slot = (lax.axis_index("wave") * n_lev + lev_idx) * per_dev
    my_waves = lax.dynamic_slice_in_dim(slot_wave, first_slot, per_dev)
    degree = jnp.arange(waves, dtype=jnp.int32)
    live_k = degree[None, :] <= trunc_top - my_waves[:, None]
    even_mask = (live_k & (degree[None, :] % 2 == 0))[:, None, :]
    odd_mask = (live_k & (degree[None, :] % 2 == 1))[:, None, :]
    zeros = jnp.zeros_like(legendre)
    leg2 = jnp.concatenate(
        [jnp.where(even_mask, legendre, zeros), jnp.where(odd_mask, legendre, zeros)], 1
    )
    sums = jnp.einsum("lscfk,sjk->sclfj", gathered, leg2, preferred_element_type=jnp.float32)
    sums = sums.reshape(per_dev, 2, fields, 2, nlath)
    north = band_rows < nlath
    lat_idx = jnp.where(north, band_rows, band_rows - nlath)
    parity_sign = jnp.where(north, 1.0, -1.0).astype(jnp.float32)
    fourier = (sums[:, :, :, 0][..., lat_idx] + parity_sign * sums[:, :, :, 1][..., lat_idx]).astype(
        jnp.bfloat16
    )
    rows = band_rows.shape[0]
    fpg = fields // n_g
    fourier = fourier.reshape(per_dev, 2, n_g, fpg, n_wave, n_r, rows_per_dev)
    fourier = jnp.transpose(fourier, (4, 2, 5, 1, 3, 6, 0))
    fourier = fourier.reshape(n_wave * n_g * n_r, 2, fpg, rows_per_dev, per_dev)
    banded = lax.all_to_all(
        fourier, ("wave", "lev_g", "lev_r"), split_axis=0, concat_axis=0, tiled=True
    )
    banded = jnp.transpose(banded, (1, 2, 3, 0, 4)).reshape(2, fpg, rows_per_dev, -1)
    wave_idx = jnp.arange(waves, dtype=jnp.int32)
    onehot = (slot_wave[:, None] == wave_idx[None, :]).astype(jnp.bfloat16)
    coef = jnp.einsum("cfrs,sm->cfrm", banded, onehot, preferred_element_type=jnp.float32)
    keep = 2 * wave_idx[None, :] < row_points[:, None]
    factor = jnp.where(keep, jnp.where(wave_idx[None, :] == 0, 1.0, 2.0), 0.0).astype(jnp.float32)
    coef = (coef * factor[None, None]).astype(jnp.bfloat16)
    coef_rows = jnp.moveaxis(coef, 2, 0)
    if rows_per_dev == 1:
        grid = row_synthesis(coef_rows[0], *(t[0] for t in tables), row_points[0])[None]
    else:
        grid = lax.map(lambda item: row_synthesis(*item), (coef_rows,) + tuple(tables) + (row_points,))
    lon = grid.shape[-1]
    fpd = fpg // n_r
    grid = grid.reshape(rows_per_dev, n_r, fpd, lon)
    me = lax.axis_index("lev_r")
    got = []
    for d in range(n_r):
        piece = lax.dynamic_index_in_dim(grid, (me + d) % n_r, 1, keepdims=False)
        if d > 0:
            piece = lax.ppermute(piece, "lev_r", [(j, (j + d) % n_r) for j in range(n_r)])
        got.append(piece)
    got = jnp.stack(got, 0)
    order = (me - jnp.arange(n_r, dtype=jnp.int32)) % n_r
    grid = jnp.take(got, order, axis=0)
    return grid.reshape(n_r * rows_per_dev, fpd, lon)


def solution(mesh):
    def run(spec, legendre, slot_wave, row_lons, band_rows):
        n_wave = mesh.shape["wave"]
        n_lev = mesh.shape["lev"]
        rows_w = band_rows.shape[0] // n_wave
        if n_lev >= rows_w:
            n_r = rows_w
            rows_per_dev = 1
        else:
            n_r = n_lev
            rows_per_dev = rows_w // n_lev
        n_g = n_lev // n_r
        devs = np.asarray(mesh.devices).reshape(n_wave, n_g, n_r)
        mesh2 = Mesh(devs, ("wave", "lev_g", "lev_r"))
        lev = ("lev_g", "lev_r")
        fn = jax.shard_map(
            lambda *a: on_device(*a, rows_per_dev=rows_per_dev),
            mesh=mesh2,
            in_specs=(P("wave", None, lev, None), P(("wave",) + lev, None, None), P(), P(), P()),
            out_specs=P("wave", lev, None),
            check_vma=False,
        )
        return fn(spec, legendre, slot_wave, row_lons, band_rows)

    return run
```

```python
import math

import jax
import jax.numpy as jnp
import numpy as np
from jax import lax
from jax.sharding import Mesh
from jax.sharding import PartitionSpec as P


def angles(remainder, points):
    return 2.0 * math.pi * remainder.astype(jnp.float32) / points.astype(jnp.float32)


def cmul(x, y):
    return x[0] * y[0] - x[1] * y[1], x[0] * y[1] + x[1] * y[0]


def bit_powers(bases, count):
    j = jnp.arange(count, dtype=jnp.int32)[None, :, None]
    c = jnp.ones((bases[0][0].shape[0], count, bases[0][0].shape[1]), jnp.float32)
    s = jnp.zeros_like(c)
    for k, (bc, bs) in enumerate(bases):
        bit = (j >> k) & 1 == 1
        c, s = cmul((c, s), (jnp.where(bit, bc[:, None], 1.0), jnp.where(bit, bs[:, None], 0.0)))
    return c, s


def outer(first, second):
    c0, s0 = first
    c1, s1 = second
    cos = c1[:, :, None] * c0[:, None] - s1[:, :, None] * s0[:, None]
    sin = s1[:, :, None] * c0[:, None] + c1[:, :, None] * s0[:, None]
    shape = (cos.shape[0], -1, cos.shape[-1])
    return cos.reshape(shape), sin.reshape(shape)


def rows_tables(points, waves):
    ablocks = waves // 64
    lon_len = 20 + 4 * (waves - 1)
    lon_idx = jnp.arange(lon_len, dtype=jnp.int32)
    pts = points[:, None]
    steps = jnp.array([1, 64], dtype=jnp.int32)[:, None, None]
    theta = angles(steps * lon_idx[None, None, :] % pts[None], pts[None])
    dc, ds = lax.optimization_barrier((jnp.cos(theta), jnp.sin(theta)))
    sq = [(dc[0], ds[0])]
    while len(sq) < 6:
        sq.append(cmul(sq[-1], sq[-1]))
    lo = bit_powers(sq[:3], 8)
    hi = bit_powers(sq[3:6], 8)
    c0, s0 = (jnp.swapaxes(x, 1, 2)[:, :, None, :] for x in lo)
    c1, s1 = (jnp.swapaxes(x, 1, 2)[:, :, :, None] for x in hi)
    rows_n, lon_n = c0.shape[0], c0.shape[1]
    cos_t = (c1 * c0 - s1 * s0).astype(jnp.bfloat16).reshape(rows_n, lon_n, 64)
    sin_t = (s1 * c0 + c1 * s0).astype(jnp.bfloat16).reshape(rows_n, lon_n, 64)
    rhs = jnp.concatenate([cos_t, sin_t], -1)
    sq = [(dc[1], ds[1])]
    while len(sq) < 5:
        sq.append(cmul(sq[-1], sq[-1]))
    n_a1 = -(-ablocks // 4)
    p0 = bit_powers(sq[:2], 4)
    p1 = bit_powers(sq[2:5], n_a1)
    return rhs, p0, p1


def rows_synthesis(coef, rhs, p0, p1, points):
    rows = coef.shape[0]
    fields = coef.shape[2]
    waves = coef.shape[3]
    ablocks = waves // 64
    lon_idx = jnp.arange(rhs.shape[1], dtype=jnp.int32)
    blocks = coef.reshape(rows, 2, fields, ablocks, 64)
    c0 = blocks[:, 0]
    c1 = blocks[:, 1]
    lhs = jnp.stack(
        [jnp.concatenate([c0, -c1], -1), jnp.concatenate([c1, c0], -1)], 1
    )
    part = jnp.einsum("rdfab,rib->rdfai", lhs, rhs, preferred_element_type=jnp.float32)
    cosp, sinp = outer(p0, p1)
    cosp = cosp[:, :ablocks]
    sinp = sinp[:, :ablocks]
    total = jnp.sum(part[:, 0] * cosp[:, None] - part[:, 1] * sinp[:, None], axis=2)
    return jnp.where(lon_idx[None, None, :] < points[:, None, None], total, jnp.zeros_like(total))


def on_device(spec, legendre, slot_wave, row_lons, band_rows, rows_per_dev):
    n_wave = lax.axis_size("wave")
    n_g = lax.axis_size("lev_g")
    n_r = lax.axis_size("lev_r")
    n_lev = n_g * n_r
    per_dev = legendre.shape[0]
    nlath = legendre.shape[1]
    waves = spec.shape[-1]
    trunc_top = waves - 1
    lev_idx = lax.axis_index("lev_g") * n_r + lax.axis_index("lev_r")
    spec_v = spec.reshape((n_lev, per_dev) + spec.shape[1:])
    gathered = lax.all_to_all(spec_v, ("lev_g", "lev_r"), split_axis=0, concat_axis=0, tiled=True)
    fields = gathered.shape[3] * n_lev
    first_row = (lax.axis_index("wave") * n_r + lax.axis_index("lev_r")) * rows_per_dev
    my_rows = lax.dynamic_slice_in_dim(band_rows, first_row, rows_per_dev)
    row_points = row_lons[my_rows]
    tables = rows_tables(row_points, waves)
    gathered, tables = lax.optimization_barrier((gathered, tables))
    first_slot = (lax.axis_index("wave") * n_lev + lev_idx) * per_dev
    my_waves = lax.dynamic_slice_in_dim(slot_wave, first_slot, per_dev)
    degree = jnp.arange(waves, dtype=jnp.int32)
    live_k = degree[None, :] <= trunc_top - my_waves[:, None]
    even_mask = (live_k & (degree[None, :] % 2 == 0))[:, None, :]
    odd_mask = (live_k & (degree[None, :] % 2 == 1))[:, None, :]
    zeros = jnp.zeros_like(legendre)
    leg2 = jnp.concatenate(
        [jnp.where(even_mask, legendre, zeros), jnp.where(odd_mask, legendre, zeros)], 1
    )
    sums = jnp.einsum("lscfk,sjk->sclfj", gathered, leg2, preferred_element_type=jnp.float32)
    sums = sums.reshape(per_dev, 2, fields, 2, nlath)
    north = band_rows < nlath
    lat_idx = jnp.where(north, band_rows, band_rows - nlath)
    parity_sign = jnp.where(north, 1.0, -1.0).astype(jnp.float32)
    fourier = (sums[:, :, :, 0][..., lat_idx] + parity_sign * sums[:, :, :, 1][..., lat_idx]).astype(
        jnp.bfloat16
    )
    rows = band_rows.shape[0]
    fpg = fields // n_g
    fourier = fourier.reshape(per_dev, 2, n_g, fpg, n_wave, n_r, rows_per_dev)
    fourier = jnp.transpose(fourier, (4, 2, 5, 1, 3, 6, 0))
    fourier = fourier.reshape(n_wave * n_g * n_r, 2, fpg, rows_per_dev, per_dev)
    banded = lax.all_to_all(
        fourier, ("wave", "lev_g", "lev_r"), split_axis=0, concat_axis=0, tiled=True
    )
    banded = jnp.transpose(banded, (1, 2, 3, 0, 4)).reshape(2, fpg, rows_per_dev, -1)
    wave_idx = jnp.arange(waves, dtype=jnp.int32)
    onehot = (slot_wave[:, None] == wave_idx[None, :]).astype(jnp.bfloat16)
    coef = jnp.einsum("cfrs,sm->cfrm", banded, onehot, preferred_element_type=jnp.float32)
    keep = 2 * wave_idx[None, :] < row_points[:, None]
    factor = jnp.where(keep, jnp.where(wave_idx[None, :] == 0, 1.0, 2.0), 0.0).astype(jnp.float32)
    coef = (coef * factor[None, None]).astype(jnp.bfloat16)
    coef_rows = jnp.moveaxis(coef, 2, 0)
    rhs_all, (p0c, p0s), (p1c, p1s) = tables
    half = rows_per_dev // 2 if rows_per_dev % 2 == 0 else rows_per_dev
    outs = []
    for h in range(0, rows_per_dev, half):
        sl = slice(h, h + half)
        piece = (coef_rows[sl], rhs_all[sl], (p0c[sl], p0s[sl]), (p1c[sl], p1s[sl]), row_points[sl])
        if outs:
            outs[-1], piece = lax.optimization_barrier((outs[-1], piece))
        outs.append(rows_synthesis(*piece))
    grid = jnp.concatenate(outs, 0) if len(outs) > 1 else outs[0]
    lon = grid.shape[-1]
    fpd = fpg // n_r
    if n_r > 1:
        grid = grid.reshape(rows_per_dev, n_r, fpd, lon)
        grid = lax.all_to_all(grid, "lev_r", split_axis=1, concat_axis=0, tiled=True)
    return grid.reshape(n_r * rows_per_dev, fpd, lon)


def solution(mesh):
    def run(spec, legendre, slot_wave, row_lons, band_rows):
        n_wave = mesh.shape["wave"]
        n_lev = mesh.shape["lev"]
        rows_w = band_rows.shape[0] // n_wave
        n_r = 1
        rows_per_dev = rows_w
        n_g = n_lev // n_r
        devs = np.asarray(mesh.devices).reshape(n_wave, n_g, n_r)
        mesh2 = Mesh(devs, ("wave", "lev_g", "lev_r"))
        lev = ("lev_g", "lev_r")
        fn = jax.shard_map(
            lambda *a: on_device(*a, rows_per_dev=rows_per_dev),
            mesh=mesh2,
            in_specs=(P("wave", None, lev, None), P(("wave",) + lev, None, None), P(), P(), P()),
            out_specs=P("wave", lev, None),
            check_vma=False,
        )
        return fn(spec, legendre, slot_wave, row_lons, band_rows)

    return run
```

```python
import math

import jax
import jax.numpy as jnp
import numpy as np
from jax import lax
from jax.sharding import Mesh
from jax.sharding import PartitionSpec as P


def angles(remainder, points):
    return 2.0 * math.pi * remainder.astype(jnp.float32) / points.astype(jnp.float32)


def trig_pair(step, lon_idx, points, count):
    mult = jnp.arange(count, dtype=jnp.int32)[None, :, None] * step
    pts = points[:, None, None]
    theta = angles(mult * lon_idx[None, None, :] % pts, pts)
    return jnp.cos(theta), jnp.sin(theta)


def compose(first, second):
    c0, s0 = first
    c1, s1 = second
    cos = c1[:, :, None] * c0[:, None] - s1[:, :, None] * s0[:, None]
    sin = s1[:, :, None] * c0[:, None] + c1[:, :, None] * s0[:, None]
    shape = (cos.shape[0], -1, cos.shape[-1])
    return cos.reshape(shape), sin.reshape(shape)


def rows_tables(points, waves):
    ablocks = waves // 64
    lon_len = 20 + 4 * (waves - 1)
    lon_idx = jnp.arange(lon_len, dtype=jnp.int32)
    cos_t, sin_t = compose(trig_pair(1, lon_idx, points, 8), trig_pair(8, lon_idx, points, 8))
    rhs = jnp.concatenate([cos_t.astype(jnp.bfloat16), sin_t.astype(jnp.bfloat16)], 1)
    n_a1 = -(-ablocks // 4)
    cosp, sinp = compose(
        trig_pair(64, lon_idx, points, 4), trig_pair(256, lon_idx, points, n_a1)
    )
    return rhs, cosp[:, :ablocks], sinp[:, :ablocks]


def row_synthesis(coef_row, rhs, cosp, sinp, points):
    fields = coef_row.shape[1]
    waves = coef_row.shape[2]
    ablocks = waves // 64
    lon_idx = jnp.arange(rhs.shape[-1], dtype=jnp.int32)
    blocks = coef_row.reshape(2, fields, ablocks, 64)
    c0 = blocks[0]
    c1 = blocks[1]
    lhs = jnp.stack(
        [jnp.concatenate([c0, -c1], -1), jnp.concatenate([c1, c0], -1)], 0
    )
    part = jnp.einsum("dfab,bi->dfai", lhs, rhs, preferred_element_type=jnp.float32)
    total = jnp.sum(part[0] * cosp[None] - part[1] * sinp[None], axis=1)
    return jnp.where(lon_idx[None, :] < points, total, jnp.zeros_like(total))


def on_device(spec, legendre, slot_wave, row_lons, band_rows, rows_per_dev):
    n_wave = lax.axis_size("wave")
    n_g = lax.axis_size("lev_g")
    n_r = lax.axis_size("lev_r")
    n_lev = n_g * n_r
    per_dev = legendre.shape[0]
    nlath = legendre.shape[1]
    waves = spec.shape[-1]
    trunc_top = waves - 1
    lev_idx = lax.axis_index("lev_g") * n_r + lax.axis_index("lev_r")
    spec_v = spec.reshape((n_lev, per_dev) + spec.shape[1:])
    gathered = lax.all_to_all(spec_v, ("lev_g", "lev_r"), split_axis=0, concat_axis=0, tiled=True)
    fields = gathered.shape[3] * n_lev
    first_row = (lax.axis_index("wave") * n_r + lax.axis_index("lev_r")) * rows_per_dev
    my_rows = lax.dynamic_slice_in_dim(band_rows, first_row, rows_per_dev)
    row_points = row_lons[my_rows]
    if rows_per_dev <= 2:
        tables = rows_tables(row_points, waves)
    else:
        tables = lax.map(lambda p: tuple(t[0] for t in rows_tables(p[None], waves)), row_points)
    gathered, tables = lax.optimization_barrier((gathered, tables))
    first_slot = (lax.axis_index("wave") * n_lev + lev_idx) * per_dev
    my_waves = lax.dynamic_slice_in_dim(slot_wave, first_slot, per_dev)
    degree = jnp.arange(waves, dtype=jnp.int32)
    live_k = degree[None, :] <= trunc_top - my_waves[:, None]
    even_mask = (live_k & (degree[None, :] % 2 == 0))[:, None, :]
    odd_mask = (live_k & (degree[None, :] % 2 == 1))[:, None, :]
    zeros = jnp.zeros_like(legendre)
    leg2 = jnp.concatenate(
        [jnp.where(even_mask, legendre, zeros), jnp.where(odd_mask, legendre, zeros)], 1
    )
    sums = jnp.einsum("lscfk,sjk->sclfj", gathered, leg2, preferred_element_type=jnp.float32)
    sums = sums.reshape(per_dev, 2, fields, 2, nlath)
    north = band_rows < nlath
    lat_idx = jnp.where(north, band_rows, band_rows - nlath)
    parity_sign = jnp.where(north, 1.0, -1.0).astype(jnp.float32)
    fourier = (sums[:, :, :, 0][..., lat_idx] + parity_sign * sums[:, :, :, 1][..., lat_idx]).astype(
        jnp.bfloat16
    )
    rows = band_rows.shape[0]
    fpg = fields // n_g
    fourier = fourier.reshape(per_dev, 2, n_g, fpg, n_wave, n_r, rows_per_dev)
    fourier = jnp.transpose(fourier, (4, 2, 5, 1, 3, 6, 0))
    fourier = fourier.reshape(n_wave * n_g * n_r, 2, fpg, rows_per_dev, per_dev)
    banded = lax.all_to_all(
        fourier, ("wave", "lev_g", "lev_r"), split_axis=0, concat_axis=0, tiled=True
    )
    banded = jnp.transpose(banded, (1, 2, 3, 0, 4)).reshape(2, fpg, rows_per_dev, -1)
    wave_idx = jnp.arange(waves, dtype=jnp.int32)
    onehot = (slot_wave[:, None] == wave_idx[None, :]).astype(jnp.bfloat16)
    coef = jnp.einsum("cfrs,sm->cfrm", banded, onehot, preferred_element_type=jnp.float32)
    keep = 2 * wave_idx[None, :] < row_points[:, None]
    factor = jnp.where(keep, jnp.where(wave_idx[None, :] == 0, 1.0, 2.0), 0.0).astype(jnp.float32)
    coef = (coef * factor[None, None]).astype(jnp.bfloat16)
    coef_rows = jnp.moveaxis(coef, 2, 0)
    if rows_per_dev == 1:
        grid = row_synthesis(coef_rows[0], *(t[0] for t in tables), row_points[0])[None]
    elif rows_per_dev <= 2:
        grid = jnp.stack(
            [
                row_synthesis(coef_rows[t], *(x[t] for x in tables), row_points[t])
                for t in range(rows_per_dev)
            ],
            0,
        )
    else:
        grid = lax.map(lambda item: row_synthesis(*item), (coef_rows,) + tuple(tables) + (row_points,))
    lon = grid.shape[-1]
    fpd = fpg // n_r
    grid = grid.reshape(rows_per_dev, n_r, fpd, lon)
    grid = lax.all_to_all(grid, "lev_r", split_axis=1, concat_axis=0, tiled=True)
    return grid.reshape(n_r * rows_per_dev, fpd, lon)


def solution(mesh):
    def run(spec, legendre, slot_wave, row_lons, band_rows):
        n_wave = mesh.shape["wave"]
        n_lev = mesh.shape["lev"]
        rows_w = band_rows.shape[0] // n_wave
        rows_per_dev = 2 if rows_w % 2 == 0 and n_lev % (rows_w // 2) == 0 else 1
        if n_lev < rows_w // rows_per_dev:
            rows_per_dev = rows_w // n_lev
        n_r = rows_w // rows_per_dev
        n_g = n_lev // n_r
        devs = np.asarray(mesh.devices).reshape(n_wave, n_g, n_r)
        mesh2 = Mesh(devs, ("wave", "lev_g", "lev_r"))
        lev = ("lev_g", "lev_r")
        fn = jax.shard_map(
            lambda *a: on_device(*a, rows_per_dev=rows_per_dev),
            mesh=mesh2,
            in_specs=(P("wave", None, lev, None), P(("wave",) + lev, None, None), P(), P(), P()),
            out_specs=P("wave", lev, None),
            check_vma=False,
        )
        return fn(spec, legendre, slot_wave, row_lons, band_rows)

    return run
```

```python
import math

import jax
import jax.numpy as jnp
import numpy as np
from jax import lax
from jax.sharding import Mesh
from jax.sharding import PartitionSpec as P


def angles(remainder, points):
    return 2.0 * math.pi * remainder.astype(jnp.float32) / points.astype(jnp.float32)


def trig_pair(step, lon_idx, points, count):
    mult = jnp.arange(count, dtype=jnp.int32)[:, None] * step
    theta = angles(mult * lon_idx[None, :] % points, points)
    return jnp.cos(theta), jnp.sin(theta)


def compose(first, second):
    c0, s0 = first
    c1, s1 = second
    cos = c1[:, None] * c0[None] - s1[:, None] * s0[None]
    sin = s1[:, None] * c0[None] + c1[:, None] * s0[None]
    return cos.reshape(-1, cos.shape[-1]), sin.reshape(-1, sin.shape[-1])


def row_synthesis(coef_row, points):
    fields = coef_row.shape[1]
    waves = coef_row.shape[2]
    ablocks = waves // 64
    lon_len = 20 + 4 * (waves - 1)
    lon_idx = jnp.arange(lon_len, dtype=jnp.int32)
    cos_t, sin_t = compose(trig_pair(1, lon_idx, points, 8), trig_pair(8, lon_idx, points, 8))
    cosb = cos_t.astype(jnp.bfloat16)
    sinb = sin_t.astype(jnp.bfloat16)
    n_a1 = -(-ablocks // 4)
    cosp, sinp = compose(
        trig_pair(64, lon_idx, points, 4), trig_pair(256, lon_idx, points, n_a1)
    )
    cosp = cosp[:ablocks]
    sinp = sinp[:ablocks]
    blocks = coef_row.reshape(2, fields, ablocks, 64)
    c0 = blocks[0]
    c1 = blocks[1]
    lhs = jnp.stack(
        [jnp.concatenate([c0, -c1], -1), jnp.concatenate([c1, c0], -1)], 0
    )
    rhs = jnp.concatenate([cosb, sinb], 0)
    part = jnp.einsum("dfab,bi->dfai", lhs, rhs, preferred_element_type=jnp.float32)
    total = jnp.sum(part[0] * cosp[None] - part[1] * sinp[None], axis=1)
    return jnp.where(lon_idx[None, :] < points, total, jnp.zeros_like(total))


def on_device(spec, legendre, slot_wave, row_lons, band_rows, rows_per_dev):
    n_wave = lax.axis_size("wave")
    n_g = lax.axis_size("lev_g")
    n_r = lax.axis_size("lev_r")
    n_lev = n_g * n_r
    per_dev = legendre.shape[0]
    nlath = legendre.shape[1]
    waves = spec.shape[-1]
    trunc_top = waves - 1
    lev_idx = lax.axis_index("lev_g") * n_r + lax.axis_index("lev_r")
    spec_v = spec.reshape((n_lev, per_dev) + spec.shape[1:])
    gathered = lax.all_to_all(spec_v, ("lev_g", "lev_r"), split_axis=0, concat_axis=0, tiled=True)
    fields = gathered.shape[3] * n_lev
    first_slot = (lax.axis_index("wave") * n_lev + lev_idx) * per_dev
    my_waves = lax.dynamic_slice_in_dim(slot_wave, first_slot, per_dev)
    degree = jnp.arange(waves, dtype=jnp.int32)
    live_k = degree[None, :] <= trunc_top - my_waves[:, None]
    north = band_rows < nlath
    lat_idx = jnp.where(north, band_rows, band_rows - nlath)
    parity_sign = jnp.where(north, 1.0, -1.0).astype(jnp.bfloat16)
    even_k = (degree % 2 == 0)[None, None, :]
    factor = jnp.where(
        live_k[:, None, :], jnp.where(even_k, jnp.bfloat16(1), parity_sign[None, :, None]), jnp.bfloat16(0)
    )
    leg_rows = jnp.take(legendre, lat_idx, axis=1) * factor
    sums = jnp.einsum("lscfk,spk->sclfp", gathered, leg_rows, preferred_element_type=jnp.float32)
    fourier = sums.reshape(per_dev, 2, fields, band_rows.shape[0]).astype(jnp.bfloat16)
    rows = band_rows.shape[0]
    fpg = fields // n_g
    fourier = fourier.reshape(per_dev, 2, n_g, fpg, n_wave, n_r, rows_per_dev)
    fourier = jnp.transpose(fourier, (4, 2, 5, 1, 3, 6, 0))
    fourier = fourier.reshape(n_wave * n_g * n_r, 2, fpg, rows_per_dev, per_dev)
    banded = lax.all_to_all(
        fourier, ("wave", "lev_g", "lev_r"), split_axis=0, concat_axis=0, tiled=True
    )
    banded = jnp.transpose(banded, (1, 2, 3, 0, 4)).reshape(2, fpg, rows_per_dev, -1)
    wave_idx = jnp.arange(waves, dtype=jnp.int32)
    onehot = (slot_wave[:, None] == wave_idx[None, :]).astype(jnp.bfloat16)
    coef = jnp.einsum("cfrs,sm->cfrm", banded, onehot, preferred_element_type=jnp.float32)
    first_row = (lax.axis_index("wave") * n_r + lax.axis_index("lev_r")) * rows_per_dev
    my_rows = lax.dynamic_slice_in_dim(band_rows, first_row, rows_per_dev)
    row_points = row_lons[my_rows]
    keep = 2 * wave_idx[None, :] < row_points[:, None]
    factor = jnp.where(keep, jnp.where(wave_idx[None, :] == 0, 1.0, 2.0), 0.0).astype(jnp.float32)
    coef = (coef * factor[None, None]).astype(jnp.bfloat16)
    coef_rows = jnp.moveaxis(coef, 2, 0)
    if rows_per_dev == 1:
        grid = row_synthesis(coef_rows[0], row_points[0])[None]
    else:
        grid = lax.map(lambda item: row_synthesis(item[0], item[1]), (coef_rows, row_points))
    lon = grid.shape[-1]
    fpd = fpg // n_r
    grid = grid.reshape(rows_per_dev, n_r, fpd, lon)
    grid = lax.all_to_all(grid, "lev_r", split_axis=1, concat_axis=0, tiled=True)
    return grid.reshape(n_r * rows_per_dev, fpd, lon)


def solution(mesh):
    def run(spec, legendre, slot_wave, row_lons, band_rows):
        n_wave = mesh.shape["wave"]
        n_lev = mesh.shape["lev"]
        rows_w = band_rows.shape[0] // n_wave
        if n_lev >= rows_w:
            n_r = rows_w
            rows_per_dev = 1
        else:
            n_r = n_lev
            rows_per_dev = rows_w // n_lev
        n_g = n_lev // n_r
        devs = np.asarray(mesh.devices).reshape(n_wave, n_g, n_r)
        mesh2 = Mesh(devs, ("wave", "lev_g", "lev_r"))
        lev = ("lev_g", "lev_r")
        fn = jax.shard_map(
            lambda *a: on_device(*a, rows_per_dev=rows_per_dev),
            mesh=mesh2,
            in_specs=(P("wave", None, lev, None), P(("wave",) + lev, None, None), P(), P(), P()),
            out_specs=P("wave", lev, None),
            check_vma=False,
        )
        return fn(spec, legendre, slot_wave, row_lons, band_rows)

    return run
```

```python
import math

import jax
import jax.numpy as jnp
import numpy as np
from jax import lax
from jax.experimental import pallas as pl
from jax.sharding import Mesh
from jax.sharding import PartitionSpec as P


def angles(remainder, points):
    return 2.0 * math.pi * remainder.astype(jnp.float32) / points.astype(jnp.float32)


def trig_pair(step, lon_idx, points, count):
    mult = jnp.arange(count, dtype=jnp.int32)[:, None] * step
    theta = angles(mult * lon_idx[None, :] % points, points)
    return jnp.cos(theta), jnp.sin(theta)


def compose(first, second):
    c0, s0 = first
    c1, s1 = second
    cos = c1[:, None] * c0[None] - s1[:, None] * s0[None]
    sin = s1[:, None] * c0[None] + c1[:, None] * s0[None]
    return cos.reshape(-1, cos.shape[-1]), sin.reshape(-1, sin.shape[-1])


def row_tables(points, waves):
    ablocks = waves // 64
    lon_len = 20 + 4 * (waves - 1)
    lon_idx = jnp.arange(lon_len, dtype=jnp.int32)
    cos_t, sin_t = compose(trig_pair(1, lon_idx, points, 8), trig_pair(8, lon_idx, points, 8))
    rhs = jnp.concatenate([cos_t.astype(jnp.bfloat16), sin_t.astype(jnp.bfloat16)], 0)
    n_a1 = -(-ablocks // 4)
    cosp, sinp = compose(
        trig_pair(64, lon_idx, points, 4), trig_pair(256, lon_idx, points, n_a1)
    )
    return rhs, cosp[:ablocks], sinp[:ablocks]


def synth_kernel(lhs_ref, rhs_ref, cos_ref, sin_ref, o_ref):
    fields = o_ref.shape[0]
    part = jnp.dot(lhs_ref[...], rhs_ref[...], preferred_element_type=jnp.float32)
    acc = jnp.zeros(o_ref.shape, jnp.float32)
    for a in range(cos_ref.shape[0]):
        re = part[2 * a * fields:(2 * a + 1) * fields]
        im = part[(2 * a + 1) * fields:(2 * a + 2) * fields]
        acc = acc + re * cos_ref[a:a + 1, :] - im * sin_ref[a:a + 1, :]
    o_ref[...] = acc


def row_synthesis(coef_row, rhs, cosp, sinp, points):
    fields = coef_row.shape[1]
    waves = coef_row.shape[2]
    ablocks = waves // 64
    lon = rhs.shape[-1]
    lon_idx = jnp.arange(lon, dtype=jnp.int32)
    blocks = coef_row.reshape(2, fields, ablocks, 64)
    c0 = blocks[0]
    c1 = blocks[1]
    lhs = jnp.stack(
        [jnp.concatenate([c0, -c1], -1), jnp.concatenate([c1, c0], -1)], 0
    )
    lhs = jnp.transpose(lhs, (2, 0, 1, 3)).reshape(ablocks * 2 * fields, 128)
    tile = 512
    total = pl.pallas_call(
        synth_kernel,
        grid=(pl.cdiv(lon, tile),),
        in_specs=[
            pl.BlockSpec((ablocks * 2 * fields, 128), lambda i: (0, 0)),
            pl.BlockSpec((128, tile), lambda i: (0, i)),
            pl.BlockSpec((ablocks, tile), lambda i: (0, i)),
            pl.BlockSpec((ablocks, tile), lambda i: (0, i)),
        ],
        out_specs=pl.BlockSpec((fields, tile), lambda i: (0, i)),
        out_shape=jax.ShapeDtypeStruct((fields, lon), jnp.float32),
    )(lhs, rhs, cosp, sinp)
    return jnp.where(lon_idx[None, :] < points, total, jnp.zeros_like(total))


def on_device(spec, legendre, slot_wave, row_lons, band_rows, rows_per_dev):
    n_wave = lax.axis_size("wave")
    n_g = lax.axis_size("lev_g")
    n_r = lax.axis_size("lev_r")
    n_lev = n_g * n_r
    per_dev = legendre.shape[0]
    nlath = legendre.shape[1]
    waves = spec.shape[-1]
    trunc_top = waves - 1
    lev_idx = lax.axis_index("lev_g") * n_r + lax.axis_index("lev_r")
    spec_v = spec.reshape((n_lev, per_dev) + spec.shape[1:])
    gathered = lax.all_to_all(spec_v, ("lev_g", "lev_r"), split_axis=0, concat_axis=0, tiled=True)
    fields = gathered.shape[3] * n_lev
    first_row = (lax.axis_index("wave") * n_r + lax.axis_index("lev_r")) * rows_per_dev
    my_rows = lax.dynamic_slice_in_dim(band_rows, first_row, rows_per_dev)
    row_points = row_lons[my_rows]
    if rows_per_dev == 1:
        tables = tuple(t[None] for t in row_tables(row_points[0], waves))
    else:
        tables = lax.map(lambda p: row_tables(p, waves), row_points)
    gathered, tables = lax.optimization_barrier((gathered, tables))
    first_slot = (lax.axis_index("wave") * n_lev + lev_idx) * per_dev
    my_waves = lax.dynamic_slice_in_dim(slot_wave, first_slot, per_dev)
    degree = jnp.arange(waves, dtype=jnp.int32)
    live_k = degree[None, :] <= trunc_top - my_waves[:, None]
    even_mask = (live_k & (degree[None, :] % 2 == 0))[:, None, :]
    odd_mask = (live_k & (degree[None, :] % 2 == 1))[:, None, :]
    zeros = jnp.zeros_like(legendre)
    leg2 = jnp.concatenate(
        [jnp.where(even_mask, legendre, zeros), jnp.where(odd_mask, legendre, zeros)], 1
    )
    sums = jnp.einsum("lscfk,sjk->sclfj", gathered, leg2, preferred_element_type=jnp.float32)
    sums = sums.reshape(per_dev, 2, fields, 2, nlath)
    north = band_rows < nlath
    lat_idx = jnp.where(north, band_rows, band_rows - nlath)
    parity_sign = jnp.where(north, 1.0, -1.0).astype(jnp.float32)
    fourier = (sums[:, :, :, 0][..., lat_idx] + parity_sign * sums[:, :, :, 1][..., lat_idx]).astype(
        jnp.bfloat16
    )
    rows = band_rows.shape[0]
    fpg = fields // n_g
    fourier = fourier.reshape(per_dev, 2, n_g, fpg, n_wave, n_r, rows_per_dev)
    fourier = jnp.transpose(fourier, (4, 2, 5, 1, 3, 6, 0))
    fourier = fourier.reshape(n_wave * n_g * n_r, 2, fpg, rows_per_dev, per_dev)
    banded = lax.all_to_all(
        fourier, ("wave", "lev_g", "lev_r"), split_axis=0, concat_axis=0, tiled=True
    )
    banded = jnp.transpose(banded, (1, 2, 3, 0, 4)).reshape(2, fpg, rows_per_dev, -1)
    wave_idx = jnp.arange(waves, dtype=jnp.int32)
    onehot = (slot_wave[:, None] == wave_idx[None, :]).astype(jnp.bfloat16)
    coef = jnp.einsum("cfrs,sm->cfrm", banded, onehot, preferred_element_type=jnp.float32)
    keep = 2 * wave_idx[None, :] < row_points[:, None]
    factor = jnp.where(keep, jnp.where(wave_idx[None, :] == 0, 1.0, 2.0), 0.0).astype(jnp.float32)
    coef = (coef * factor[None, None]).astype(jnp.bfloat16)
    coef_rows = jnp.moveaxis(coef, 2, 0)
    if rows_per_dev == 1:
        grid = row_synthesis(coef_rows[0], *(t[0] for t in tables), row_points[0])[None]
    else:
        grid = lax.map(lambda item: row_synthesis(*item), (coef_rows,) + tuple(tables) + (row_points,))
    lon = grid.shape[-1]
    fpd = fpg // n_r
    grid = grid.reshape(rows_per_dev, n_r, fpd, lon)
    grid = lax.all_to_all(grid, "lev_r", split_axis=1, concat_axis=0, tiled=True)
    return grid.reshape(n_r * rows_per_dev, fpd, lon)


def solution(mesh):
    def run(spec, legendre, slot_wave, row_lons, band_rows):
        n_wave = mesh.shape["wave"]
        n_lev = mesh.shape["lev"]
        rows_w = band_rows.shape[0] // n_wave
        if n_lev >= rows_w:
            n_r = rows_w
            rows_per_dev = 1
        else:
            n_r = n_lev
            rows_per_dev = rows_w // n_lev
        n_g = n_lev // n_r
        devs = np.asarray(mesh.devices).reshape(n_wave, n_g, n_r)
        mesh2 = Mesh(devs, ("wave", "lev_g", "lev_r"))
        lev = ("lev_g", "lev_r")
        fn = jax.shard_map(
            lambda *a: on_device(*a, rows_per_dev=rows_per_dev),
            mesh=mesh2,
            in_specs=(P("wave", None, lev, None), P(("wave",) + lev, None, None), P(), P(), P()),
            out_specs=P("wave", lev, None),
            check_vma=False,
        )
        return fn(spec, legendre, slot_wave, row_lons, band_rows)

    return run
```

```python
import math

import jax
import jax.numpy as jnp
import numpy as np
from jax import lax
from jax.experimental import pallas as pl
from jax.sharding import Mesh
from jax.sharding import PartitionSpec as P


def angles(remainder, points):
    return 2.0 * math.pi * remainder.astype(jnp.float32) / points.astype(jnp.float32)


def trig_pair(step, lon_idx, points, count):
    mult = jnp.arange(count, dtype=jnp.int32)[:, None] * step
    theta = angles(mult * lon_idx[None, :] % points, points)
    return jnp.cos(theta), jnp.sin(theta)


def compose(first, second):
    c0, s0 = first
    c1, s1 = second
    cos = c1[:, None] * c0[None] - s1[:, None] * s0[None]
    sin = s1[:, None] * c0[None] + c1[:, None] * s0[None]
    return cos.reshape(-1, cos.shape[-1]), sin.reshape(-1, sin.shape[-1])


def row_tables(points, waves):
    ablocks = waves // 64
    lon_len = 20 + 4 * (waves - 1)
    lon_idx = jnp.arange(lon_len, dtype=jnp.int32)
    cos_t, sin_t = compose(trig_pair(1, lon_idx, points, 8), trig_pair(8, lon_idx, points, 8))
    rhs = jnp.concatenate([cos_t.astype(jnp.bfloat16), sin_t.astype(jnp.bfloat16)], 0)
    n_a1 = -(-ablocks // 4)
    cosp, sinp = compose(
        trig_pair(64, lon_idx, points, 4), trig_pair(256, lon_idx, points, n_a1)
    )
    return rhs, cosp[:ablocks], sinp[:ablocks]


def synth_kernel(lhs_ref, rhs_ref, cos_ref, sin_ref, o_ref):
    fields = o_ref.shape[0]
    part = jnp.dot(lhs_ref[...], rhs_ref[...], preferred_element_type=jnp.float32)
    acc = jnp.zeros(o_ref.shape, jnp.float32)
    for a in range(cos_ref.shape[0]):
        re = part[2 * a * fields:(2 * a + 1) * fields]
        im = part[(2 * a + 1) * fields:(2 * a + 2) * fields]
        acc = acc + re * cos_ref[a:a + 1, :] - im * sin_ref[a:a + 1, :]
    o_ref[...] = acc


def row_synthesis(coef_row, rhs, cosp, sinp, points):
    fields = coef_row.shape[1]
    waves = coef_row.shape[2]
    ablocks = waves // 64
    lon = rhs.shape[-1]
    lon_idx = jnp.arange(lon, dtype=jnp.int32)
    blocks = coef_row.reshape(2, fields, ablocks, 64)
    c0 = blocks[0]
    c1 = blocks[1]
    lhs = jnp.stack(
        [jnp.concatenate([c0, -c1], -1), jnp.concatenate([c1, c0], -1)], 0
    )
    lhs = jnp.transpose(lhs, (2, 0, 1, 3)).reshape(ablocks * 2 * fields, 128)
    tile = 1024
    total = pl.pallas_call(
        synth_kernel,
        grid=(pl.cdiv(lon, tile),),
        in_specs=[
            pl.BlockSpec((ablocks * 2 * fields, 128), lambda i: (0, 0)),
            pl.BlockSpec((128, tile), lambda i: (0, i)),
            pl.BlockSpec((ablocks, tile), lambda i: (0, i)),
            pl.BlockSpec((ablocks, tile), lambda i: (0, i)),
        ],
        out_specs=pl.BlockSpec((fields, tile), lambda i: (0, i)),
        out_shape=jax.ShapeDtypeStruct((fields, lon), jnp.float32),
    )(lhs, rhs, cosp, sinp)
    return jnp.where(lon_idx[None, :] < points, total, jnp.zeros_like(total))


def on_device(spec, legendre, slot_wave, row_lons, band_rows, rows_per_dev):
    n_wave = lax.axis_size("wave")
    n_g = lax.axis_size("lev_g")
    n_r = lax.axis_size("lev_r")
    n_lev = n_g * n_r
    per_dev = legendre.shape[0]
    nlath = legendre.shape[1]
    waves = spec.shape[-1]
    trunc_top = waves - 1
    lev_idx = lax.axis_index("lev_g") * n_r + lax.axis_index("lev_r")
    spec_v = spec.reshape((n_lev, per_dev) + spec.shape[1:])
    gathered = lax.all_to_all(spec_v, ("lev_g", "lev_r"), split_axis=0, concat_axis=0, tiled=True)
    fields = gathered.shape[3] * n_lev
    first_row = (lax.axis_index("wave") * n_r + lax.axis_index("lev_r")) * rows_per_dev
    my_rows = lax.dynamic_slice_in_dim(band_rows, first_row, rows_per_dev)
    row_points = row_lons[my_rows]
    if rows_per_dev == 1:
        tables = tuple(t[None] for t in row_tables(row_points[0], waves))
    else:
        tables = lax.map(lambda p: row_tables(p, waves), row_points)
    gathered, tables = lax.optimization_barrier((gathered, tables))
    first_slot = (lax.axis_index("wave") * n_lev + lev_idx) * per_dev
    my_waves = lax.dynamic_slice_in_dim(slot_wave, first_slot, per_dev)
    degree = jnp.arange(waves, dtype=jnp.int32)
    live_k = degree[None, :] <= trunc_top - my_waves[:, None]
    even_mask = (live_k & (degree[None, :] % 2 == 0))[:, None, :]
    odd_mask = (live_k & (degree[None, :] % 2 == 1))[:, None, :]
    zeros = jnp.zeros_like(legendre)
    leg2 = jnp.concatenate(
        [jnp.where(even_mask, legendre, zeros), jnp.where(odd_mask, legendre, zeros)], 1
    )
    sums = jnp.einsum("lscfk,sjk->sclfj", gathered, leg2, preferred_element_type=jnp.float32)
    sums = sums.reshape(per_dev, 2, fields, 2, nlath)
    north = band_rows < nlath
    lat_idx = jnp.where(north, band_rows, band_rows - nlath)
    parity_sign = jnp.where(north, 1.0, -1.0).astype(jnp.float32)
    fourier = (sums[:, :, :, 0][..., lat_idx] + parity_sign * sums[:, :, :, 1][..., lat_idx]).astype(
        jnp.bfloat16
    )
    rows = band_rows.shape[0]
    fpg = fields // n_g
    fourier = fourier.reshape(per_dev, 2, n_g, fpg, n_wave, n_r, rows_per_dev)
    fourier = jnp.transpose(fourier, (4, 2, 5, 1, 3, 6, 0))
    fourier = fourier.reshape(n_wave * n_g * n_r, 2, fpg, rows_per_dev, per_dev)
    banded = lax.all_to_all(
        fourier, ("wave", "lev_g", "lev_r"), split_axis=0, concat_axis=0, tiled=True
    )
    banded = jnp.transpose(banded, (1, 2, 3, 0, 4)).reshape(2, fpg, rows_per_dev, -1)
    wave_idx = jnp.arange(waves, dtype=jnp.int32)
    onehot = (slot_wave[:, None] == wave_idx[None, :]).astype(jnp.bfloat16)
    coef = jnp.einsum("cfrs,sm->cfrm", banded, onehot, preferred_element_type=jnp.float32)
    keep = 2 * wave_idx[None, :] < row_points[:, None]
    factor = jnp.where(keep, jnp.where(wave_idx[None, :] == 0, 1.0, 2.0), 0.0).astype(jnp.float32)
    coef = (coef * factor[None, None]).astype(jnp.bfloat16)
    coef_rows = jnp.moveaxis(coef, 2, 0)
    if rows_per_dev == 1:
        grid = row_synthesis(coef_rows[0], *(t[0] for t in tables), row_points[0])[None]
    else:
        grid = lax.map(lambda item: row_synthesis(*item), (coef_rows,) + tuple(tables) + (row_points,))
    lon = grid.shape[-1]
    fpd = fpg // n_r
    grid = grid.reshape(rows_per_dev, n_r, fpd, lon)
    grid = lax.all_to_all(grid, "lev_r", split_axis=1, concat_axis=0, tiled=True)
    return grid.reshape(n_r * rows_per_dev, fpd, lon)


def solution(mesh):
    def run(spec, legendre, slot_wave, row_lons, band_rows):
        n_wave = mesh.shape["wave"]
        n_lev = mesh.shape["lev"]
        rows_w = band_rows.shape[0] // n_wave
        if n_lev >= rows_w:
            n_r = rows_w
            rows_per_dev = 1
        else:
            n_r = n_lev
            rows_per_dev = rows_w // n_lev
        n_g = n_lev // n_r
        devs = np.asarray(mesh.devices).reshape(n_wave, n_g, n_r)
        mesh2 = Mesh(devs, ("wave", "lev_g", "lev_r"))
        lev = ("lev_g", "lev_r")
        fn = jax.shard_map(
            lambda *a: on_device(*a, rows_per_dev=rows_per_dev),
            mesh=mesh2,
            in_specs=(P("wave", None, lev, None), P(("wave",) + lev, None, None), P(), P(), P()),
            out_specs=P("wave", lev, None),
            check_vma=False,
        )
        return fn(spec, legendre, slot_wave, row_lons, band_rows)

    return run
```

```python
import math

import jax
import jax.numpy as jnp
import numpy as np
from jax import lax
from jax.experimental import pallas as pl
from jax.sharding import Mesh
from jax.sharding import PartitionSpec as P


def angles(remainder, points):
    return 2.0 * math.pi * remainder.astype(jnp.float32) / points.astype(jnp.float32)


def trig_pair(step, lon_idx, points, count):
    mult = jnp.arange(count, dtype=jnp.int32)[:, None] * step
    theta = angles(mult * lon_idx[None, :] % points, points)
    return jnp.cos(theta), jnp.sin(theta)


def compose(first, second):
    c0, s0 = first
    c1, s1 = second
    cos = c1[:, None] * c0[None] - s1[:, None] * s0[None]
    sin = s1[:, None] * c0[None] + c1[:, None] * s0[None]
    return cos.reshape(-1, cos.shape[-1]), sin.reshape(-1, sin.shape[-1])


def row_tables(points, waves):
    ablocks = waves // 64
    lon_len = 20 + 4 * (waves - 1)
    lon_idx = jnp.arange(lon_len, dtype=jnp.int32)
    cos_t, sin_t = compose(trig_pair(1, lon_idx, points, 8), trig_pair(8, lon_idx, points, 8))
    rhs = jnp.concatenate([cos_t.astype(jnp.bfloat16), sin_t.astype(jnp.bfloat16)], 0)
    n_a1 = -(-ablocks // 4)
    cosp, sinp = compose(
        trig_pair(64, lon_idx, points, 4), trig_pair(256, lon_idx, points, n_a1)
    )
    return rhs, cosp[:ablocks], sinp[:ablocks]


def synth_kernel(lhs_ref, rhs_ref, cos_ref, sin_ref, o_ref):
    fields = o_ref.shape[0]
    rhs = rhs_ref[...]
    acc = jnp.zeros(o_ref.shape, jnp.float32)
    for a in range(cos_ref.shape[0]):
        part = jnp.dot(
            lhs_ref[2 * a * fields:(2 * a + 2) * fields, :], rhs, preferred_element_type=jnp.float32
        )
        acc = acc + part[:fields] * cos_ref[a:a + 1, :] - part[fields:] * sin_ref[a:a + 1, :]
    o_ref[...] = acc


def row_synthesis(coef_row, rhs, cosp, sinp, points):
    fields = coef_row.shape[1]
    waves = coef_row.shape[2]
    ablocks = waves // 64
    lon = rhs.shape[-1]
    lon_idx = jnp.arange(lon, dtype=jnp.int32)
    blocks = coef_row.reshape(2, fields, ablocks, 64)
    c0 = blocks[0]
    c1 = blocks[1]
    lhs = jnp.stack(
        [jnp.concatenate([c0, -c1], -1), jnp.concatenate([c1, c0], -1)], 0
    )
    lhs = jnp.transpose(lhs, (2, 0, 1, 3)).reshape(ablocks * 2 * fields, 128)
    tile = 1024
    total = pl.pallas_call(
        synth_kernel,
        grid=(pl.cdiv(lon, tile),),
        in_specs=[
            pl.BlockSpec((ablocks * 2 * fields, 128), lambda i: (0, 0)),
            pl.BlockSpec((128, tile), lambda i: (0, i)),
            pl.BlockSpec((ablocks, tile), lambda i: (0, i)),
            pl.BlockSpec((ablocks, tile), lambda i: (0, i)),
        ],
        out_specs=pl.BlockSpec((fields, tile), lambda i: (0, i)),
        out_shape=jax.ShapeDtypeStruct((fields, lon), jnp.float32),
    )(lhs, rhs, cosp, sinp)
    return jnp.where(lon_idx[None, :] < points, total, jnp.zeros_like(total))


def on_device(spec, legendre, slot_wave, row_lons, band_rows, rows_per_dev):
    n_wave = lax.axis_size("wave")
    n_g = lax.axis_size("lev_g")
    n_r = lax.axis_size("lev_r")
    n_lev = n_g * n_r
    per_dev = legendre.shape[0]
    nlath = legendre.shape[1]
    waves = spec.shape[-1]
    trunc_top = waves - 1
    lev_idx = lax.axis_index("lev_g") * n_r + lax.axis_index("lev_r")
    spec_v = spec.reshape((n_lev, per_dev) + spec.shape[1:])
    gathered = lax.all_to_all(spec_v, ("lev_g", "lev_r"), split_axis=0, concat_axis=0, tiled=True)
    fields = gathered.shape[3] * n_lev
    first_row = (lax.axis_index("wave") * n_r + lax.axis_index("lev_r")) * rows_per_dev
    my_rows = lax.dynamic_slice_in_dim(band_rows, first_row, rows_per_dev)
    row_points = row_lons[my_rows]
    if rows_per_dev == 1:
        tables = tuple(t[None] for t in row_tables(row_points[0], waves))
    else:
        tables = lax.map(lambda p: row_tables(p, waves), row_points)
    gathered, tables = lax.optimization_barrier((gathered, tables))
    first_slot = (lax.axis_index("wave") * n_lev + lev_idx) * per_dev
    my_waves = lax.dynamic_slice_in_dim(slot_wave, first_slot, per_dev)
    degree = jnp.arange(waves, dtype=jnp.int32)
    live_k = degree[None, :] <= trunc_top - my_waves[:, None]
    even_mask = (live_k & (degree[None, :] % 2 == 0))[:, None, :]
    odd_mask = (live_k & (degree[None, :] % 2 == 1))[:, None, :]
    zeros = jnp.zeros_like(legendre)
    leg2 = jnp.concatenate(
        [jnp.where(even_mask, legendre, zeros), jnp.where(odd_mask, legendre, zeros)], 1
    )
    sums = jnp.einsum("lscfk,sjk->sclfj", gathered, leg2, preferred_element_type=jnp.float32)
    sums = sums.reshape(per_dev, 2, fields, 2, nlath)
    north = band_rows < nlath
    lat_idx = jnp.where(north, band_rows, band_rows - nlath)
    parity_sign = jnp.where(north, 1.0, -1.0).astype(jnp.float32)
    fourier = (sums[:, :, :, 0][..., lat_idx] + parity_sign * sums[:, :, :, 1][..., lat_idx]).astype(
        jnp.bfloat16
    )
    rows = band_rows.shape[0]
    fpg = fields // n_g
    fourier = fourier.reshape(per_dev, 2, n_g, fpg, n_wave, n_r, rows_per_dev)
    fourier = jnp.transpose(fourier, (4, 2, 5, 1, 3, 6, 0))
    fourier = fourier.reshape(n_wave * n_g * n_r, 2, fpg, rows_per_dev, per_dev)
    banded = lax.all_to_all(
        fourier, ("wave", "lev_g", "lev_r"), split_axis=0, concat_axis=0, tiled=True
    )
    banded = jnp.transpose(banded, (1, 2, 3, 0, 4)).reshape(2, fpg, rows_per_dev, -1)
    wave_idx = jnp.arange(waves, dtype=jnp.int32)
    onehot = (slot_wave[:, None] == wave_idx[None, :]).astype(jnp.bfloat16)
    coef = jnp.einsum("cfrs,sm->cfrm", banded, onehot, preferred_element_type=jnp.float32)
    keep = 2 * wave_idx[None, :] < row_points[:, None]
    factor = jnp.where(keep, jnp.where(wave_idx[None, :] == 0, 1.0, 2.0), 0.0).astype(jnp.float32)
    coef = (coef * factor[None, None]).astype(jnp.bfloat16)
    coef_rows = jnp.moveaxis(coef, 2, 0)
    if rows_per_dev == 1:
        grid = row_synthesis(coef_rows[0], *(t[0] for t in tables), row_points[0])[None]
    else:
        grid = lax.map(lambda item: row_synthesis(*item), (coef_rows,) + tuple(tables) + (row_points,))
    lon = grid.shape[-1]
    fpd = fpg // n_r
    grid = grid.reshape(rows_per_dev, n_r, fpd, lon)
    grid = lax.all_to_all(grid, "lev_r", split_axis=1, concat_axis=0, tiled=True)
    return grid.reshape(n_r * rows_per_dev, fpd, lon)


def solution(mesh):
    def run(spec, legendre, slot_wave, row_lons, band_rows):
        n_wave = mesh.shape["wave"]
        n_lev = mesh.shape["lev"]
        rows_w = band_rows.shape[0] // n_wave
        if n_lev >= rows_w:
            n_r = rows_w
            rows_per_dev = 1
        else:
            n_r = n_lev
            rows_per_dev = rows_w // n_lev
        n_g = n_lev // n_r
        devs = np.asarray(mesh.devices).reshape(n_wave, n_g, n_r)
        mesh2 = Mesh(devs, ("wave", "lev_g", "lev_r"))
        lev = ("lev_g", "lev_r")
        fn = jax.shard_map(
            lambda *a: on_device(*a, rows_per_dev=rows_per_dev),
            mesh=mesh2,
            in_specs=(P("wave", None, lev, None), P(("wave",) + lev, None, None), P(), P(), P()),
            out_specs=P("wave", lev, None),
            check_vma=False,
        )
        return fn(spec, legendre, slot_wave, row_lons, band_rows)

    return run
```

```python
import math

import jax
import jax.numpy as jnp
import numpy as np
from jax import lax
from jax.sharding import Mesh
from jax.sharding import PartitionSpec as P


def angles(remainder, points):
    return 2.0 * math.pi * remainder.astype(jnp.float32) / points.astype(jnp.float32)


def trig_pair(step, lon_idx, points, count):
    mult = jnp.arange(count, dtype=jnp.int32)[:, None] * step
    theta = angles(mult * lon_idx[None, :] % points, points)
    return jnp.cos(theta), jnp.sin(theta)


def compose(first, second):
    c0, s0 = first
    c1, s1 = second
    cos = c1[:, None] * c0[None] - s1[:, None] * s0[None]
    sin = s1[:, None] * c0[None] + c1[:, None] * s0[None]
    return cos.reshape(-1, cos.shape[-1]), sin.reshape(-1, sin.shape[-1])


def row_synthesis(coef_row, points):
    fields = coef_row.shape[1]
    waves = coef_row.shape[2]
    ablocks = waves // 64
    lon_len = 20 + 4 * (waves - 1)
    lon_idx = jnp.arange(lon_len, dtype=jnp.int32)
    cos_t, sin_t = compose(trig_pair(1, lon_idx, points, 8), trig_pair(8, lon_idx, points, 8))
    cosb = cos_t.astype(jnp.bfloat16)
    sinb = sin_t.astype(jnp.bfloat16)
    n_a1 = -(-ablocks // 4)
    cosp, sinp = compose(
        trig_pair(64, lon_idx, points, 4), trig_pair(256, lon_idx, points, n_a1)
    )
    cosp = cosp[:ablocks]
    sinp = sinp[:ablocks]
    blocks = coef_row.reshape(2, fields, ablocks, 64)
    c0 = blocks[0]
    c1 = blocks[1]
    lhs = jnp.stack(
        [jnp.concatenate([c0, -c1], -1), jnp.concatenate([c1, c0], -1)], 0
    )
    rhs = jnp.concatenate([cosb, sinb], 0)
    part = jnp.einsum("dfab,bi->dfai", lhs, rhs, preferred_element_type=jnp.float32)
    total = jnp.sum(part[0] * cosp[None] - part[1] * sinp[None], axis=1)
    return jnp.where(lon_idx[None, :] < points, total, jnp.zeros_like(total))


def on_device(spec, legendre, slot_wave, row_lons, band_rows, rows_per_dev):
    n_wave = lax.axis_size("wave")
    n_g = lax.axis_size("lev_g")
    n_r = lax.axis_size("lev_r")
    n_lev = n_g * n_r
    per_dev = legendre.shape[0]
    nlath = legendre.shape[1]
    waves = spec.shape[-1]
    trunc_top = waves - 1
    lev_idx = lax.axis_index("lev_g") * n_r + lax.axis_index("lev_r")
    spec_v = spec.reshape((n_lev, per_dev) + spec.shape[1:])
    gathered = lax.all_to_all(spec_v, ("lev_g", "lev_r"), split_axis=0, concat_axis=0, tiled=True)
    fields = gathered.shape[3] * n_lev
    first_slot = (lax.axis_index("wave") * n_lev + lev_idx) * per_dev
    my_waves = lax.dynamic_slice_in_dim(slot_wave, first_slot, per_dev)
    degree = jnp.arange(waves, dtype=jnp.int32)
    live_k = degree[None, :] <= trunc_top - my_waves[:, None]
    even_mask = (live_k & (degree[None, :] % 2 == 0))[:, None, :]
    odd_mask = (live_k & (degree[None, :] % 2 == 1))[:, None, :]
    zeros = jnp.zeros_like(legendre)
    leg2 = jnp.concatenate(
        [jnp.where(even_mask, legendre, zeros), jnp.where(odd_mask, legendre, zeros)], 1
    )
    sums = jnp.einsum("lscfk,sjk->jclfs", gathered, leg2, preferred_element_type=jnp.float32)
    sums = sums.reshape(2 * nlath, 2, fields, per_dev)
    north = band_rows < nlath
    lat_idx = jnp.where(north, band_rows, band_rows - nlath)
    parity_sign = jnp.where(north, 1.0, -1.0).astype(jnp.float32)
    fourier = (sums[lat_idx] + parity_sign[:, None, None, None] * sums[nlath + lat_idx]).astype(
        jnp.bfloat16
    )
    fpg = fields // n_g
    fourier = fourier.reshape(n_wave, n_r, rows_per_dev, 2, n_g, fpg, per_dev)
    fourier = jnp.transpose(fourier, (0, 4, 1, 3, 5, 2, 6))
    fourier = fourier.reshape(n_wave * n_g * n_r, 2, fpg, rows_per_dev, per_dev)
    banded = lax.all_to_all(
        fourier, ("wave", "lev_g", "lev_r"), split_axis=0, concat_axis=0, tiled=True
    )
    banded = jnp.transpose(banded, (1, 2, 3, 0, 4)).reshape(2, fpg, rows_per_dev, -1)
    wave_idx = jnp.arange(waves, dtype=jnp.int32)
    onehot = (slot_wave[:, None] == wave_idx[None, :]).astype(jnp.bfloat16)
    coef = jnp.einsum("cfrs,sm->cfrm", banded, onehot, preferred_element_type=jnp.float32)
    first_row = (lax.axis_index("wave") * n_r + lax.axis_index("lev_r")) * rows_per_dev
    my_rows = lax.dynamic_slice_in_dim(band_rows, first_row, rows_per_dev)
    row_points = row_lons[my_rows]
    keep = 2 * wave_idx[None, :] < row_points[:, None]
    factor = jnp.where(keep, jnp.where(wave_idx[None, :] == 0, 1.0, 2.0), 0.0).astype(jnp.float32)
    coef = (coef * factor[None, None]).astype(jnp.bfloat16)
    coef_rows = jnp.moveaxis(coef, 2, 0)
    if rows_per_dev == 1:
        grid = row_synthesis(coef_rows[0], row_points[0])[None]
    else:
        grid = lax.map(lambda item: row_synthesis(item[0], item[1]), (coef_rows, row_points))
    lon = grid.shape[-1]
    fpd = fpg // n_r
    grid = grid.reshape(rows_per_dev, n_r, fpd, lon)
    grid = lax.all_to_all(grid, "lev_r", split_axis=1, concat_axis=0, tiled=True)
    return grid.reshape(n_r * rows_per_dev, fpd, lon)


def solution(mesh):
    def run(spec, legendre, slot_wave, row_lons, band_rows):
        n_wave = mesh.shape["wave"]
        n_lev = mesh.shape["lev"]
        rows_w = band_rows.shape[0] // n_wave
        if n_lev >= rows_w:
            n_r = rows_w
            rows_per_dev = 1
        else:
            n_r = n_lev
            rows_per_dev = rows_w // n_lev
        n_g = n_lev // n_r
        devs = np.asarray(mesh.devices).reshape(n_wave, n_g, n_r)
        mesh2 = Mesh(devs, ("wave", "lev_g", "lev_r"))
        lev = ("lev_g", "lev_r")
        fn = jax.shard_map(
            lambda *a: on_device(*a, rows_per_dev=rows_per_dev),
            mesh=mesh2,
            in_specs=(P("wave", None, lev, None), P(("wave",) + lev, None, None), P(), P(), P()),
            out_specs=P("wave", lev, None),
            check_vma=False,
        )
        return fn(spec, legendre, slot_wave, row_lons, band_rows)

    return run
```

```python
import math

import jax
import jax.numpy as jnp
import numpy as np
from jax import lax
from jax.sharding import Mesh
from jax.sharding import PartitionSpec as P


def angles(remainder, points):
    return 2.0 * math.pi * remainder.astype(jnp.float32) / points.astype(jnp.float32)


def trig_pair(step, lon_idx, points, count):
    mult = jnp.arange(count, dtype=jnp.int32)[:, None] * step
    theta = angles(mult * lon_idx[None, :] % points, points)
    return jnp.cos(theta), jnp.sin(theta)


def compose(first, second):
    c0, s0 = first
    c1, s1 = second
    cos = c1[:, None] * c0[None] - s1[:, None] * s0[None]
    sin = s1[:, None] * c0[None] + c1[:, None] * s0[None]
    return cos.reshape(-1, cos.shape[-1]), sin.reshape(-1, sin.shape[-1])


def row_synthesis(coef_row, points):
    fields = coef_row.shape[1]
    waves = coef_row.shape[2]
    ablocks = waves // 64
    lon_len = 20 + 4 * (waves - 1)
    lon_idx = jnp.arange(lon_len, dtype=jnp.int32)
    cos_t, sin_t = compose(trig_pair(1, lon_idx, points, 8), trig_pair(8, lon_idx, points, 8))
    cosb = cos_t.astype(jnp.bfloat16)
    sinb = sin_t.astype(jnp.bfloat16)
    n_a1 = -(-ablocks // 4)
    cosp, sinp = compose(
        trig_pair(64, lon_idx, points, 4), trig_pair(256, lon_idx, points, n_a1)
    )
    cosp = cosp[:ablocks]
    sinp = sinp[:ablocks]
    blocks = coef_row.reshape(2, fields, ablocks, 64)
    c0 = blocks[0]
    c1 = blocks[1]
    lhs = jnp.stack(
        [jnp.concatenate([c0, -c1], -1), jnp.concatenate([c1, c0], -1)], 0
    )
    rhs = jnp.concatenate([cosb, sinb], 0)
    part = jnp.einsum("dfab,bi->dfai", lhs, rhs, preferred_element_type=jnp.float32)
    total = jnp.sum(part[0] * cosp[None] - part[1] * sinp[None], axis=1)
    return jnp.where(lon_idx[None, :] < points, total, jnp.zeros_like(total))


def on_device(spec, legendre, slot_wave, row_lons, band_rows, rows_per_dev):
    n_wave = lax.axis_size("wave")
    n_g = lax.axis_size("lev_g")
    n_r = lax.axis_size("lev_r")
    n_lev = n_g * n_r
    per_dev = legendre.shape[0]
    nlath = legendre.shape[1]
    waves = spec.shape[-1]
    trunc_top = waves - 1
    lev_idx = lax.axis_index("lev_g") * n_r + lax.axis_index("lev_r")
    spec_v = spec.reshape((n_lev, per_dev) + spec.shape[1:])
    gathered = lax.all_to_all(spec_v, ("lev_g", "lev_r"), split_axis=0, concat_axis=0, tiled=True)
    fields = gathered.shape[3] * n_lev
    first_slot = (lax.axis_index("wave") * n_lev + lev_idx) * per_dev
    my_waves = lax.dynamic_slice_in_dim(slot_wave, first_slot, per_dev)
    degree = jnp.arange(waves, dtype=jnp.int32)
    live_k = degree[None, :] <= trunc_top - my_waves[:, None]
    even_mask = (live_k & (degree[None, :] % 2 == 0))[:, None, :]
    odd_mask = (live_k & (degree[None, :] % 2 == 1))[:, None, :]
    zeros = jnp.zeros_like(legendre)
    leg2 = jnp.concatenate(
        [jnp.where(even_mask, legendre, zeros), jnp.where(odd_mask, legendre, zeros)], 1
    )
    sums = jnp.einsum("lscfk,sjk->sclfj", gathered, leg2, preferred_element_type=jnp.float32)
    sums = sums.reshape(per_dev, 2, fields, 2, nlath)
    north = band_rows < nlath
    lat_idx = jnp.where(north, band_rows, band_rows - nlath)
    parity_sign = jnp.where(north, 1.0, -1.0).astype(jnp.float32)
    fourier = (sums[:, :, :, 0][..., lat_idx] + parity_sign * sums[:, :, :, 1][..., lat_idx]).astype(
        jnp.bfloat16
    )
    rows = band_rows.shape[0]
    fpg = fields // n_g
    fourier = fourier.reshape(per_dev, 2, n_g, fpg, n_wave, n_r, rows_per_dev)
    fourier = jnp.transpose(fourier, (4, 2, 5, 1, 3, 6, 0))
    fourier = fourier.reshape(n_wave * n_g * n_r, 2, fpg, rows_per_dev, per_dev)
    banded = lax.all_to_all(
        fourier, ("wave", "lev_g", "lev_r"), split_axis=0, concat_axis=0, tiled=True
    )
    banded = jnp.transpose(banded, (1, 2, 3, 0, 4)).reshape(2, fpg, rows_per_dev, -1)
    wave_idx = jnp.arange(waves, dtype=jnp.int32)
    first_row = (lax.axis_index("wave") * n_r + lax.axis_index("lev_r")) * rows_per_dev
    my_rows = lax.dynamic_slice_in_dim(band_rows, first_row, rows_per_dev)
    row_points = row_lons[my_rows]
    keep = 2 * wave_idx[None, :] < row_points[:, None]
    factor = jnp.where(keep, jnp.where(wave_idx[None, :] == 0, 2.0, 4.0), 0.0) / 2.0
    onehot = jnp.where(
        slot_wave[None, :, None] == wave_idx[None, None, :], factor[:, None, :], 0.0
    ).astype(jnp.bfloat16)
    coef = jnp.einsum("cfrs,rsm->cfrm", banded, onehot, preferred_element_type=jnp.float32)
    coef = coef.astype(jnp.bfloat16)
    coef_rows = jnp.moveaxis(coef, 2, 0)
    if rows_per_dev == 1:
        grid = row_synthesis(coef_rows[0], row_points[0])[None]
    else:
        grid = lax.map(lambda item: row_synthesis(item[0], item[1]), (coef_rows, row_points))
    lon = grid.shape[-1]
    fpd = fpg // n_r
    grid = grid.reshape(rows_per_dev, n_r, fpd, lon)
    grid = lax.all_to_all(grid, "lev_r", split_axis=1, concat_axis=0, tiled=True)
    return grid.reshape(n_r * rows_per_dev, fpd, lon)


def solution(mesh):
    def run(spec, legendre, slot_wave, row_lons, band_rows):
        n_wave = mesh.shape["wave"]
        n_lev = mesh.shape["lev"]
        rows_w = band_rows.shape[0] // n_wave
        if n_lev >= rows_w:
            n_r = rows_w
            rows_per_dev = 1
        else:
            n_r = n_lev
            rows_per_dev = rows_w // n_lev
        n_g = n_lev // n_r
        devs = np.asarray(mesh.devices).reshape(n_wave, n_g, n_r)
        mesh2 = Mesh(devs, ("wave", "lev_g", "lev_r"))
        lev = ("lev_g", "lev_r")
        fn = jax.shard_map(
            lambda *a: on_device(*a, rows_per_dev=rows_per_dev),
            mesh=mesh2,
            in_specs=(P("wave", None, lev, None), P(("wave",) + lev, None, None), P(), P(), P()),
            out_specs=P("wave", lev, None),
            check_vma=False,
        )
        return fn(spec, legendre, slot_wave, row_lons, band_rows)

    return run
```

```python
import math

import jax
import jax.numpy as jnp
import numpy as np
from jax import lax
from jax.sharding import Mesh
from jax.sharding import PartitionSpec as P


def angles(remainder, points):
    return 2.0 * math.pi * remainder.astype(jnp.float32) / points.astype(jnp.float32)


def trig_pair(step, lon_idx, points, count):
    mult = jnp.arange(count, dtype=jnp.int32)[:, None] * step
    theta = angles(mult * lon_idx[None, :] % points, points)
    return jnp.cos(theta), jnp.sin(theta)


def compose(first, second):
    c0, s0 = first
    c1, s1 = second
    cos = c1[:, None] * c0[None] - s1[:, None] * s0[None]
    sin = s1[:, None] * c0[None] + c1[:, None] * s0[None]
    return cos.reshape(-1, cos.shape[-1]), sin.reshape(-1, sin.shape[-1])


def row_synthesis(coef_row, points):
    fields = coef_row.shape[1]
    waves = coef_row.shape[2]
    ablocks = waves // 64
    lon_len = 20 + 4 * (waves - 1)
    lon_idx = jnp.arange(lon_len, dtype=jnp.int32)
    cos_t, sin_t = compose(trig_pair(1, lon_idx, points, 8), trig_pair(8, lon_idx, points, 8))
    cosb = cos_t.astype(jnp.bfloat16)
    sinb = sin_t.astype(jnp.bfloat16)
    n_a1 = -(-ablocks // 4)
    cosp, sinp = compose(
        trig_pair(64, lon_idx, points, 4), trig_pair(256, lon_idx, points, n_a1)
    )
    cosp = cosp[:ablocks]
    sinp = sinp[:ablocks]
    blocks = coef_row.reshape(2, fields, ablocks, 64)
    c0 = blocks[0]
    c1 = blocks[1]
    lhs = jnp.stack(
        [jnp.concatenate([c0, -c1], -1), jnp.concatenate([c1, c0], -1)], 0
    )
    rhs = jnp.concatenate([cosb, sinb], 0)
    part = jnp.einsum("dfab,bi->dfai", lhs, rhs, preferred_element_type=jnp.float32)
    total = jnp.sum(part[0] * cosp[None] - part[1] * sinp[None], axis=1)
    return jnp.where(lon_idx[None, :] < points, total, jnp.zeros_like(total))


def on_device(spec, legendre, slot_wave, row_lons, band_rows, rows_per_dev):
    n_wave = lax.axis_size("wave")
    n_g = lax.axis_size("lev_g")
    n_r = lax.axis_size("lev_r")
    n_lev = n_g * n_r
    per_dev = legendre.shape[0]
    nlath = legendre.shape[1]
    waves = spec.shape[-1]
    trunc_top = waves - 1
    lev_idx = lax.axis_index("lev_g") * n_r + lax.axis_index("lev_r")
    spec_v = spec.reshape((n_lev, per_dev) + spec.shape[1:])
    gathered = lax.all_to_all(spec_v, ("lev_g", "lev_r"), split_axis=0, concat_axis=0, tiled=True)
    fields = gathered.shape[3] * n_lev
    first_slot = (lax.axis_index("wave") * n_lev + lev_idx) * per_dev
    my_waves = lax.dynamic_slice_in_dim(slot_wave, first_slot, per_dev)
    degree = jnp.arange(waves, dtype=jnp.int32)
    live_k = degree[None, :] <= trunc_top - my_waves[:, None]
    even_mask = (live_k & (degree[None, :] % 2 == 0))[:, None, :]
    odd_mask = (live_k & (degree[None, :] % 2 == 1))[:, None, :]
    zeros = jnp.zeros_like(legendre)
    leg2 = jnp.concatenate(
        [jnp.where(even_mask, legendre, zeros), jnp.where(odd_mask, legendre, zeros)], 1
    )
    sums = jnp.einsum("lscfk,sjk->sclfj", gathered, leg2, preferred_element_type=jnp.float32)
    sums = sums.reshape(per_dev, 2, fields, 2 * nlath)
    north = band_rows < nlath
    lat_idx = jnp.where(north, band_rows, band_rows - nlath)
    j2 = jnp.arange(2 * nlath, dtype=jnp.int32)[:, None]
    sel = jnp.where(j2 == lat_idx[None, :], 1.0, 0.0) + jnp.where(
        j2 == nlath + lat_idx[None, :], jnp.where(north, 1.0, -1.0)[None, :], 0.0
    )
    fourier = jnp.einsum(
        "scfj,jp->scfp", sums, sel, precision=lax.Precision.HIGHEST,
        preferred_element_type=jnp.float32,
    ).astype(jnp.bfloat16)
    rows = band_rows.shape[0]
    fpg = fields // n_g
    fourier = fourier.reshape(per_dev, 2, n_g, fpg, n_wave, n_r, rows_per_dev)
    fourier = jnp.transpose(fourier, (4, 2, 5, 1, 3, 6, 0))
    fourier = fourier.reshape(n_wave * n_g * n_r, 2, fpg, rows_per_dev, per_dev)
    banded = lax.all_to_all(
        fourier, ("wave", "lev_g", "lev_r"), split_axis=0, concat_axis=0, tiled=True
    )
    banded = jnp.transpose(banded, (1, 2, 3, 0, 4)).reshape(2, fpg, rows_per_dev, -1)
    wave_idx = jnp.arange(waves, dtype=jnp.int32)
    first_row = (lax.axis_index("wave") * n_r + lax.axis_index("lev_r")) * rows_per_dev
    my_rows = lax.dynamic_slice_in_dim(band_rows, first_row, rows_per_dev)
    row_points = row_lons[my_rows]
    keep = 2 * wave_idx[None, :] < row_points[:, None]
    factor = jnp.where(keep, jnp.where(wave_idx[None, :] == 0, 2.0, 4.0), 0.0) / 2.0
    onehot = jnp.where(
        slot_wave[None, :, None] == wave_idx[None, None, :], factor[:, None, :], 0.0
    ).astype(jnp.bfloat16)
    coef = jnp.einsum("cfrs,rsm->cfrm", banded, onehot, preferred_element_type=jnp.float32)
    coef = coef.astype(jnp.bfloat16)
    coef_rows = jnp.moveaxis(coef, 2, 0)
    if rows_per_dev == 1:
        grid = row_synthesis(coef_rows[0], row_points[0])[None]
    else:
        grid = lax.map(lambda item: row_synthesis(item[0], item[1]), (coef_rows, row_points))
    lon = grid.shape[-1]
    fpd = fpg // n_r
    grid = grid.reshape(rows_per_dev, n_r, fpd, lon)
    grid = lax.all_to_all(grid, "lev_r", split_axis=1, concat_axis=0, tiled=True)
    return grid.reshape(n_r * rows_per_dev, fpd, lon)


def solution(mesh):
    def run(spec, legendre, slot_wave, row_lons, band_rows):
        n_wave = mesh.shape["wave"]
        n_lev = mesh.shape["lev"]
        rows_w = band_rows.shape[0] // n_wave
        if n_lev >= rows_w:
            n_r = rows_w
            rows_per_dev = 1
        else:
            n_r = n_lev
            rows_per_dev = rows_w // n_lev
        n_g = n_lev // n_r
        devs = np.asarray(mesh.devices).reshape(n_wave, n_g, n_r)
        mesh2 = Mesh(devs, ("wave", "lev_g", "lev_r"))
        lev = ("lev_g", "lev_r")
        fn = jax.shard_map(
            lambda *a: on_device(*a, rows_per_dev=rows_per_dev),
            mesh=mesh2,
            in_specs=(P("wave", None, lev, None), P(("wave",) + lev, None, None), P(), P(), P()),
            out_specs=P("wave", lev, None),
            check_vma=False,
        )
        return fn(spec, legendre, slot_wave, row_lons, band_rows)

    return run
```

```python
import math

import jax
import jax.numpy as jnp
import numpy as np
from jax import lax
from jax.sharding import Mesh
from jax.sharding import PartitionSpec as P


def angles(remainder, points):
    return 2.0 * math.pi * remainder.astype(jnp.float32) / points.astype(jnp.float32)


def trig_pair(step, lon_idx, points, count):
    mult = jnp.arange(count, dtype=jnp.int32)[:, None] * step
    theta = angles(mult * lon_idx[None, :] % points, points)
    return jnp.cos(theta), jnp.sin(theta)


def compose(first, second):
    c0, s0 = first
    c1, s1 = second
    cos = c1[:, None] * c0[None] - s1[:, None] * s0[None]
    sin = s1[:, None] * c0[None] + c1[:, None] * s0[None]
    return cos.reshape(-1, cos.shape[-1]), sin.reshape(-1, sin.shape[-1])


def row_synthesis(coef_row, points):
    fields = coef_row.shape[1]
    waves = coef_row.shape[2]
    ablocks = waves // 64
    lon_len = 20 + 4 * (waves - 1)
    lon_idx = jnp.arange(lon_len, dtype=jnp.int32)
    cos_t, sin_t = compose(trig_pair(1, lon_idx, points, 8), trig_pair(8, lon_idx, points, 8))
    cosb = cos_t.astype(jnp.bfloat16)
    sinb = sin_t.astype(jnp.bfloat16)
    n_a1 = -(-ablocks // 4)
    cosp, sinp = compose(
        trig_pair(64, lon_idx, points, 4), trig_pair(256, lon_idx, points, n_a1)
    )
    cosp = cosp[:ablocks]
    sinp = sinp[:ablocks]
    blocks = coef_row.reshape(2, fields, ablocks, 64)
    c0 = blocks[0]
    c1 = blocks[1]
    lhs = jnp.stack(
        [jnp.concatenate([c0, -c1], -1), jnp.concatenate([c1, c0], -1)], 0
    )
    rhs = jnp.concatenate([cosb, sinb], 0)
    part = jnp.einsum("dfab,bi->dfai", lhs, rhs, preferred_element_type=jnp.float32)
    total = jnp.sum(part[0] * cosp[None] - part[1] * sinp[None], axis=1)
    return jnp.where(lon_idx[None, :] < points, total, jnp.zeros_like(total))


def on_device(spec, legendre, slot_wave, row_lons, band_rows, rows_per_dev):
    n_wave = lax.axis_size("wave")
    n_g = lax.axis_size("lev_g")
    n_r = lax.axis_size("lev_r")
    n_lev = n_g * n_r
    per_dev = legendre.shape[0]
    nlath = legendre.shape[1]
    waves = spec.shape[-1]
    trunc_top = waves - 1
    lev_idx = lax.axis_index("lev_g") * n_r + lax.axis_index("lev_r")
    spec_v = spec.reshape((n_lev, per_dev) + spec.shape[1:])
    gathered = lax.all_to_all(spec_v, ("lev_g", "lev_r"), split_axis=0, concat_axis=0, tiled=True)
    fields = gathered.shape[3] * n_lev
    first_slot = (lax.axis_index("wave") * n_lev + lev_idx) * per_dev
    my_waves = lax.dynamic_slice_in_dim(slot_wave, first_slot, per_dev)
    degree = jnp.arange(waves, dtype=jnp.int32)
    live_k = degree[None, :] <= trunc_top - my_waves[:, None]
    even_mask = (live_k & (degree[None, :] % 2 == 0))[:, None, :]
    odd_mask = (live_k & (degree[None, :] % 2 == 1))[:, None, :]
    zeros = jnp.zeros_like(legendre)
    leg2 = jnp.concatenate(
        [jnp.where(even_mask, legendre, zeros), jnp.where(odd_mask, legendre, zeros)], 1
    )
    north = band_rows < nlath
    lat_idx = jnp.where(north, band_rows, band_rows - nlath)
    j2 = jnp.arange(2 * nlath, dtype=jnp.int32)[:, None]
    sel = jnp.where(j2 == lat_idx[None, :], 1.0, 0.0) + jnp.where(
        j2 == nlath + lat_idx[None, :], jnp.where(north, 1.0, -1.0)[None, :], 0.0
    )
    leg_rows = jnp.einsum(
        "sjk,jp->spk", leg2, sel.astype(jnp.bfloat16), preferred_element_type=jnp.float32
    ).astype(jnp.bfloat16)
    sums = jnp.einsum("lscfk,spk->sclfp", gathered, leg_rows, preferred_element_type=jnp.float32)
    fourier = sums.reshape(per_dev, 2, fields, band_rows.shape[0]).astype(jnp.bfloat16)
    rows = band_rows.shape[0]
    fpg = fields // n_g
    fourier = fourier.reshape(per_dev, 2, n_g, fpg, n_wave, n_r, rows_per_dev)
    fourier = jnp.transpose(fourier, (4, 2, 5, 1, 3, 6, 0))
    fourier = fourier.reshape(n_wave * n_g * n_r, 2, fpg, rows_per_dev, per_dev)
    banded = lax.all_to_all(
        fourier, ("wave", "lev_g", "lev_r"), split_axis=0, concat_axis=0, tiled=True
    )
    banded = jnp.transpose(banded, (1, 2, 3, 0, 4)).reshape(2, fpg, rows_per_dev, -1)
    wave_idx = jnp.arange(waves, dtype=jnp.int32)
    first_row = (lax.axis_index("wave") * n_r + lax.axis_index("lev_r")) * rows_per_dev
    my_rows = lax.dynamic_slice_in_dim(band_rows, first_row, rows_per_dev)
    row_points = row_lons[my_rows]
    keep = 2 * wave_idx[None, :] < row_points[:, None]
    factor = jnp.where(keep, jnp.where(wave_idx[None, :] == 0, 2.0, 4.0), 0.0) / 2.0
    onehot = jnp.where(
        slot_wave[None, :, None] == wave_idx[None, None, :], factor[:, None, :], 0.0
    ).astype(jnp.bfloat16)
    coef = jnp.einsum("cfrs,rsm->cfrm", banded, onehot, preferred_element_type=jnp.float32)
    coef = coef.astype(jnp.bfloat16)
    coef_rows = jnp.moveaxis(coef, 2, 0)
    if rows_per_dev == 1:
        grid = row_synthesis(coef_rows[0], row_points[0])[None]
    else:
        grid = lax.map(lambda item: row_synthesis(item[0], item[1]), (coef_rows, row_points))
    lon = grid.shape[-1]
    fpd = fpg // n_r
    grid = grid.reshape(rows_per_dev, n_r, fpd, lon)
    grid = lax.all_to_all(grid, "lev_r", split_axis=1, concat_axis=0, tiled=True)
    return grid.reshape(n_r * rows_per_dev, fpd, lon)


def solution(mesh):
    def run(spec, legendre, slot_wave, row_lons, band_rows):
        n_wave = mesh.shape["wave"]
        n_lev = mesh.shape["lev"]
        rows_w = band_rows.shape[0] // n_wave
        if n_lev >= rows_w:
            n_r = rows_w
            rows_per_dev = 1
        else:
            n_r = n_lev
            rows_per_dev = rows_w // n_lev
        n_g = n_lev // n_r
        devs = np.asarray(mesh.devices).reshape(n_wave, n_g, n_r)
        mesh2 = Mesh(devs, ("wave", "lev_g", "lev_r"))
        lev = ("lev_g", "lev_r")
        fn = jax.shard_map(
            lambda *a: on_device(*a, rows_per_dev=rows_per_dev),
            mesh=mesh2,
            in_specs=(P("wave", None, lev, None), P(("wave",) + lev, None, None), P(), P(), P()),
            out_specs=P("wave", lev, None),
            check_vma=False,
        )
        return fn(spec, legendre, slot_wave, row_lons, band_rows)

    return run
```

```python
import math

import jax
import jax.numpy as jnp
import numpy as np
from jax import lax
from jax.sharding import Mesh
from jax.sharding import PartitionSpec as P


def angles(remainder, points):
    return 2.0 * math.pi * remainder.astype(jnp.float32) / points.astype(jnp.float32)


def trig_pair(step, lon_idx, points, count):
    mult = jnp.arange(count, dtype=jnp.int32)[:, None] * step
    theta = angles(mult * lon_idx[None, :] % points, points)
    return jnp.cos(theta), jnp.sin(theta)


def compose(first, second):
    c0, s0 = first
    c1, s1 = second
    cos = c1[:, None] * c0[None] - s1[:, None] * s0[None]
    sin = s1[:, None] * c0[None] + c1[:, None] * s0[None]
    return cos.reshape(-1, cos.shape[-1]), sin.reshape(-1, sin.shape[-1])


def row_synthesis(coef_row, points):
    fields = coef_row.shape[1]
    waves = coef_row.shape[2]
    ablocks = waves // 64
    lon_len = 20 + 4 * (waves - 1)
    lon_idx = jnp.arange(lon_len, dtype=jnp.int32)
    cos_t, sin_t = compose(trig_pair(1, lon_idx, points, 8), trig_pair(8, lon_idx, points, 8))
    cosb = cos_t.astype(jnp.bfloat16)
    sinb = sin_t.astype(jnp.bfloat16)
    n_a1 = -(-ablocks // 4)
    cosp, sinp = compose(
        trig_pair(64, lon_idx, points, 4), trig_pair(256, lon_idx, points, n_a1)
    )
    cosp = cosp[:ablocks]
    sinp = sinp[:ablocks]
    blocks = coef_row.reshape(2, fields, ablocks, 64)
    c0 = blocks[0]
    c1 = blocks[1]
    lhs = jnp.stack(
        [jnp.concatenate([c0, -c1], -1), jnp.concatenate([c1, c0], -1)], 0
    )
    rhs = jnp.concatenate([cosb, sinb], 0)
    part = jnp.einsum("dfab,bi->dfai", lhs, rhs, preferred_element_type=jnp.float32)
    total = jnp.sum(part[0] * cosp[None] - part[1] * sinp[None], axis=1)
    return total


def on_device(spec, legendre, slot_wave, row_lons, band_rows, rows_per_dev):
    n_wave = lax.axis_size("wave")
    n_g = lax.axis_size("lev_g")
    n_r = lax.axis_size("lev_r")
    n_lev = n_g * n_r
    per_dev = legendre.shape[0]
    nlath = legendre.shape[1]
    waves = spec.shape[-1]
    trunc_top = waves - 1
    lev_idx = lax.axis_index("lev_g") * n_r + lax.axis_index("lev_r")
    spec_v = spec.reshape((n_lev, per_dev) + spec.shape[1:])
    gathered = lax.all_to_all(spec_v, ("lev_g", "lev_r"), split_axis=0, concat_axis=0, tiled=True)
    fields = gathered.shape[3] * n_lev
    first_slot = (lax.axis_index("wave") * n_lev + lev_idx) * per_dev
    my_waves = lax.dynamic_slice_in_dim(slot_wave, first_slot, per_dev)
    degree = jnp.arange(waves, dtype=jnp.int32)
    live_k = degree[None, :] <= trunc_top - my_waves[:, None]
    even_mask = (live_k & (degree[None, :] % 2 == 0))[:, None, :]
    odd_mask = (live_k & (degree[None, :] % 2 == 1))[:, None, :]
    zeros = jnp.zeros_like(legendre)
    leg2 = jnp.concatenate(
        [jnp.where(even_mask, legendre, zeros), jnp.where(odd_mask, legendre, zeros)], 1
    )
    sums = jnp.einsum("lscfk,sjk->sclfj", gathered, leg2, preferred_element_type=jnp.float32)
    sums = sums.reshape(per_dev, 2, fields, 2 * nlath)
    north = band_rows < nlath
    lat_idx = jnp.where(north, band_rows, band_rows - nlath)
    j2 = jnp.arange(2 * nlath, dtype=jnp.int32)[:, None]
    sel = jnp.where(j2 == lat_idx[None, :], 1.0, 0.0) + jnp.where(
        j2 == nlath + lat_idx[None, :], jnp.where(north, 1.0, -1.0)[None, :], 0.0
    )
    fourier = jnp.einsum(
        "scfj,jp->scfp", sums, sel, precision=lax.Precision.HIGHEST,
        preferred_element_type=jnp.float32,
    ).astype(jnp.bfloat16)
    rows = band_rows.shape[0]
    fpg = fields // n_g
    fourier = fourier.reshape(per_dev, 2, n_g, fpg, n_wave, n_r, rows_per_dev)
    fourier = jnp.transpose(fourier, (4, 2, 5, 1, 3, 6, 0))
    fourier = fourier.reshape(n_wave * n_g * n_r, 2, fpg, rows_per_dev, per_dev)
    banded = lax.all_to_all(
        fourier, ("wave", "lev_g", "lev_r"), split_axis=0, concat_axis=0, tiled=True
    )
    banded = jnp.transpose(banded, (1, 2, 3, 0, 4)).reshape(2, fpg, rows_per_dev, -1)
    wave_idx = jnp.arange(waves, dtype=jnp.int32)
    first_row = (lax.axis_index("wave") * n_r + lax.axis_index("lev_r")) * rows_per_dev
    my_rows = lax.dynamic_slice_in_dim(band_rows, first_row, rows_per_dev)
    row_points = row_lons[my_rows]
    keep = 2 * wave_idx[None, :] < row_points[:, None]
    factor = jnp.where(keep, jnp.where(wave_idx[None, :] == 0, 2.0, 4.0), 0.0) / 2.0
    onehot = jnp.where(
        slot_wave[None, :, None] == wave_idx[None, None, :], factor[:, None, :], 0.0
    ).astype(jnp.bfloat16)
    coef = jnp.einsum("cfrs,rsm->cfrm", banded, onehot, preferred_element_type=jnp.float32)
    coef = coef.astype(jnp.bfloat16)
    coef_rows = jnp.moveaxis(coef, 2, 0)
    if rows_per_dev == 1:
        grid = row_synthesis(coef_rows[0], row_points[0])[None]
    else:
        grid = lax.map(lambda item: row_synthesis(item[0], item[1]), (coef_rows, row_points))
    lon = grid.shape[-1]
    fpd = fpg // n_r
    grid = grid.reshape(rows_per_dev, n_r, fpd, lon)
    grid = lax.all_to_all(grid, "lev_r", split_axis=1, concat_axis=0, tiled=True)
    grid = grid.reshape(n_r * rows_per_dev, fpd, lon)
    group_rows = lax.dynamic_slice_in_dim(band_rows, lax.axis_index("wave") * n_r * rows_per_dev, n_r * rows_per_dev)
    group_points = row_lons[group_rows]
    lon_idx = jnp.arange(lon, dtype=jnp.int32)
    return jnp.where(lon_idx[None, None, :] < group_points[:, None, None], grid, jnp.zeros_like(grid))


def solution(mesh):
    def run(spec, legendre, slot_wave, row_lons, band_rows):
        n_wave = mesh.shape["wave"]
        n_lev = mesh.shape["lev"]
        rows_w = band_rows.shape[0] // n_wave
        if n_lev >= rows_w:
            n_r = rows_w
            rows_per_dev = 1
        else:
            n_r = n_lev
            rows_per_dev = rows_w // n_lev
        n_g = n_lev // n_r
        devs = np.asarray(mesh.devices).reshape(n_wave, n_g, n_r)
        mesh2 = Mesh(devs, ("wave", "lev_g", "lev_r"))
        lev = ("lev_g", "lev_r")
        fn = jax.shard_map(
            lambda *a: on_device(*a, rows_per_dev=rows_per_dev),
            mesh=mesh2,
            in_specs=(P("wave", None, lev, None), P(("wave",) + lev, None, None), P(), P(), P()),
            out_specs=P("wave", lev, None),
            check_vma=False,
        )
        return fn(spec, legendre, slot_wave, row_lons, band_rows)

    return run
```
